512 devices in a mesh: blk: 256 (over z, x_hi, y, core), rep: 2 (over x_lo).
Axes of the slice: x: 4 (x_hi: 2, x_lo: 2; x = x_hi * 2 + x_lo), y: 8, z: 8, core: 2. Of those that a mesh axis runs over, the one named last changes fastest.
Arguments:
- samples: bfloat16 [8192, 16, 2048], P('blk', 'rep'), may hold values from -60 to 60, as said below
- offsets: int32 [4, 8192], P(None, 'blk'), may hold values from 0 to 31
- bad_mask: int32 [8192], P('blk'), may hold values 0 or 1
Outputs:
- correlations: float32 [8192, 4, 257], P('blk')
- mirrored: float32 [8192, 4, 257], P('blk')
The draws below stay inside these ranges and needn't reach their ends.
Inputs may be any that keep to these rules, and one draw needn't show every extreme that they name: `samples`: samples vary in scale between channels and segments; channels near one another share a delayed common source.
All inputs are finite; a program needn't handle non-finite values. No bound on the sum of `bad_mask` on one device may be relied on, other than what follows from the above.
Results may differ from the reference program's by a relative error of at most 0.0017.
Values may be sent and summed in bfloat16 or wider, within the bound.
No kernel may reach another device: no remote copies, remote signals or barrier semaphores. Data moves between devices by JAX's collectives and lax.ppermute only.
A program may use at most 64 MiB of HBM per device.

```python
import math
import jax
import jax.numpy as jnp
from jax import lax

CH_DEV = 32
NS = 2048
LAGS = 128
STOPS = 4
NF = 1024
LAGW = 257
CHANNELS = 8192
NSEG = 16
N_BLK = 256


def draw_samples(key, part):
    key_scale, key_own, key_common = jax.random.split(key, 3)
    scales = jnp.exp(jax.random.uniform(key_scale, (CHANNELS, NSEG, 1), jnp.float32, math.log(0.1), math.log(10.0)))
    own = jax.random.normal(key_own, (CHANNELS, NSEG, NS), jnp.float32)
    common = jax.random.normal(key_common, (NSEG, NS), jnp.float32)
    delays = jnp.arange(CHANNELS, dtype=jnp.int32) * 37 % 97
    where = (jnp.arange(NS, dtype=jnp.int32)[None, :] - delays[:, None]) % NS
    shared = jnp.transpose(common[:, where], (1, 0, 2))
    values = scales * (own + 0.8 * shared)
    return jnp.clip(values, -60.0, 60.0).astype(jnp.bfloat16)


def place_ends(entries, rng, low, high):
    shape = entries.shape
    place = [jax.random.randint(jax.random.fold_in(rng, axis), (), 0, shape[axis]) for axis in range(len(shape))]
    entries = entries.at[tuple(place)].set(low)
    longest = shape.index(max(shape))
    place[longest] = (place[longest] + 1) % shape[longest]
    return entries.at[tuple(place)].set(high)


def setup_inputs(seed: int = 0) -> dict:
    splits = jax.random.split(jax.random.key(seed), 4)
    return {
        "samples": draw_samples(jax.random.fold_in(splits[3], 71), 0),
        "offsets": place_ends(jax.random.randint(splits[1], (STOPS, CHANNELS), 0, CH_DEV), jax.random.fold_in(splits[1], 1), 0, CH_DEV - 1).astype(jnp.int32),
        "bad_mask": place_ends((jax.random.randint(splits[2], (CHANNELS,), 0, 8) < 1).astype(jnp.int32), jax.random.fold_in(splits[2], 1), 0, 1),
    }


def forward_table(length):
    half_len = length // 2
    sample_idx = lax.iota(jnp.int32, length)
    bin_idx = lax.iota(jnp.int32, half_len)
    phase = sample_idx[:, None] * bin_idx[None, :] % length
    angle = phase.astype(jnp.float32) * (2.0 * math.pi / length)
    return jnp.concatenate([jnp.cos(angle), -jnp.sin(angle)], axis=1).astype(jnp.bfloat16)

def inverse_table(length, lag_half):
    half_len = length // 2
    bin_idx = lax.iota(jnp.int32, half_len)
    lag_idx = lax.iota(jnp.int32, 2 * lag_half + 1) - lag_half
    phase = bin_idx[:, None] * (lag_idx[None, :] % length) % length
    angle = phase.astype(jnp.float32) * (2.0 * math.pi / length)
    return jnp.concatenate([jnp.cos(angle), -jnp.sin(angle)], axis=0)

def whiten(spectrum, keep, half_len):
    power = lax.optimization_barrier(jnp.sum(spectrum * spectrum, axis=-1, keepdims=True)) / half_len
    return (spectrum * lax.rsqrt(power + 1e-06) * keep[:, None, None]).astype(jnp.bfloat16)

def cross_spectrum(local, partner, half_len):
    first = local.astype(jnp.float32)
    second = partner.astype(jnp.float32)
    real_a, imag_a = (first[..., :half_len], first[..., half_len:])
    real_b, imag_b = (second[..., :half_len], second[..., half_len:])
    real_sum = lax.optimization_barrier(jnp.sum(real_a * real_b + imag_a * imag_b, axis=1))
    imag_sum = lax.optimization_barrier(jnp.sum(imag_a * real_b - real_a * imag_b, axis=1))
    return jnp.concatenate([real_sum, imag_sum], axis=-1)

def reference(samples, offsets, bad_mask):
    table = forward_table(NS).astype(jnp.float32)
    back_table = inverse_table(NS, LAGS)
    keep = (1 - bad_mask).astype(jnp.float32)
    scale = 1.0 / math.sqrt(NSEG * NF)

    def one_block(block):
        start = (block * CH_DEV).astype(jnp.int32)
        rows = lax.dynamic_slice_in_dim(samples, start, CH_DEV, 0).astype(jnp.float32)
        spectrum = jnp.dot(rows.reshape(CH_DEV * NSEG, NS), table, precision=lax.Precision.HIGHEST, preferred_element_type=jnp.float32).reshape(CH_DEV, NSEG, NS)
        return whiten(spectrum, lax.dynamic_slice_in_dim(keep, start, CH_DEV, 0), NF)
    blocks = jnp.arange(N_BLK, dtype=jnp.int32)
    white = lax.map(one_block, blocks).reshape(CHANNELS, NSEG, NS)

    def block_corr(block):
        start = (block * CH_DEV).astype(jnp.int32)
        local = lax.dynamic_slice_in_dim(white, start, CH_DEV, 0)
        pieces = []
        for stop in range(1, STOPS + 1):
            source = ((block - stop) % N_BLK * CH_DEV).astype(jnp.int32)
            remote = lax.dynamic_slice_in_dim(white, source, CH_DEV, 0)
            picks = lax.dynamic_slice_in_dim(offsets[stop - 1], start, CH_DEV, 0)
            partner = jnp.take(remote, picks, axis=0)
            pieces.append(cross_spectrum(local, partner, NF))
        cross = jnp.stack(pieces, axis=1)
        corr = jnp.dot(cross.reshape(CH_DEV * STOPS, NS), back_table, precision=lax.Precision.HIGHEST, preferred_element_type=jnp.float32)
        return corr.reshape(CH_DEV, STOPS, LAGW) * scale
    correlations = lax.map(block_corr, blocks).reshape(CHANNELS, STOPS, LAGW)
    stop_idx = jnp.arange(STOPS, dtype=jnp.int32)
    owner = (jnp.arange(CHANNELS, dtype=jnp.int32)[:, None] + (stop_idx[None, :] + 1) * CH_DEV) % CHANNELS
    mirrored = correlations[owner, stop_idx[None, :], :][:, :, ::-1]
    return (correlations, mirrored)
```

```python
import math

import jax
import jax.numpy as jnp
from jax import lax
from jax.sharding import PartitionSpec as P

LAGS = 128


def shifted(x, axis, by):
    length = lax.axis_size(axis)
    return lax.ppermute(x, axis, [(i, (i + by) % length) for i in range(length)])


def swapped(x, axis):
    length = lax.axis_size(axis)
    return lax.ppermute(x, axis, [(i, i ^ 1) for i in range(length)])


def cos_sin(phase, length):
    angle = phase.astype(jnp.float32) * (2.0 * math.pi / length)
    return jnp.cos(angle), jnp.sin(angle)


def forward_table(length):
    half_len = length // 2
    lo_len = 64
    hi_len = length // lo_len
    bin_idx = lax.iota(jnp.int32, half_len)
    hi_idx = lax.iota(jnp.int32, hi_len) * lo_len
    lo_idx = lax.iota(jnp.int32, lo_len)
    cos_hi, sin_hi = cos_sin(hi_idx[:, None] * bin_idx[None, :] % length, length)
    cos_lo, sin_lo = cos_sin(lo_idx[:, None] * bin_idx[None, :] % length, length)
    cos_hi, sin_hi = cos_hi[:, None, :], sin_hi[:, None, :]
    cos_lo, sin_lo = cos_lo[None, :, :], sin_lo[None, :, :]
    cos_t = cos_hi * cos_lo - sin_hi * sin_lo
    sin_t = sin_hi * cos_lo + cos_hi * sin_lo
    table = jnp.concatenate([cos_t, -sin_t], axis=-1)
    return table.reshape(length, length).astype(jnp.bfloat16)


def inverse_table(length, lag_half):
    half_len = length // 2
    lo_len = 32
    hi_len = half_len // lo_len
    lag_idx = (lax.iota(jnp.int32, 2 * lag_half + 1) - lag_half) % length
    hi_idx = lax.iota(jnp.int32, hi_len) * lo_len
    lo_idx = lax.iota(jnp.int32, lo_len)
    cos_hi, sin_hi = cos_sin(hi_idx[:, None] * lag_idx[None, :] % length, length)
    cos_lo, sin_lo = cos_sin(lo_idx[:, None] * lag_idx[None, :] % length, length)
    cos_hi, sin_hi = cos_hi[:, None, :], sin_hi[:, None, :]
    cos_lo, sin_lo = cos_lo[None, :, :], sin_lo[None, :, :]
    cos_t = (cos_hi * cos_lo - sin_hi * sin_lo).reshape(half_len, -1)
    sin_t = (sin_hi * cos_lo + cos_hi * sin_lo).reshape(half_len, -1)
    return jnp.concatenate([cos_t, -sin_t], axis=0)


def whiten(spectrum, keep, half_len):
    power = jnp.sum(spectrum * spectrum, axis=-1, keepdims=True) / half_len
    return (spectrum * lax.rsqrt(power + 1e-06) * keep[:, None, None]).astype(jnp.bfloat16)


def cross_spectrum(local, partner, half_len):
    first = local.astype(jnp.float32)
    second = partner.astype(jnp.float32)
    real_a, imag_a = (first[..., :half_len], first[..., half_len:])
    real_b, imag_b = (second[..., :half_len], second[..., half_len:])
    real_sum = jnp.sum(real_a * real_b + imag_a * imag_b, axis=1)
    imag_sum = jnp.sum(imag_a * real_b - real_a * imag_b, axis=1)
    return jnp.concatenate([real_sum, imag_sum], axis=-1)


def on_device(samples, offsets, bad_mask):
    channels, segments, length = samples.shape
    half_len = length // 2
    stops = offsets.shape[0]
    spectrum = jnp.dot(
        samples.reshape(channels * segments, length),
        forward_table(length),
        preferred_element_type=jnp.float32,
    ).reshape(channels, segments, length)
    keep = (1 - bad_mask).astype(jnp.float32)
    white = whiten(spectrum, keep, half_len)
    split = segments // 2
    ahead = white[:, :split]
    behind = white[:, split:]
    moving_ahead = ahead
    moving_behind = behind
    moving_offsets = offsets
    own_pieces = []
    later_pieces = []
    for stop in range(1, stops + 1):
        moving_ahead = shifted(moving_ahead, "blk", 1)
        moving_behind = shifted(moving_behind, "blk", -1)
        moving_offsets = shifted(moving_offsets, "blk", -1)
        partner = jnp.take(moving_ahead, offsets[stop - 1], axis=0)
        own_pieces.append(cross_spectrum(ahead, partner, half_len))
        local_partner = jnp.take(behind, moving_offsets[stop - 1], axis=0)
        later_pieces.append(cross_spectrum(moving_behind, local_partner, half_len))
    back_table = inverse_table(length, LAGS)
    pieces = jnp.stack([jnp.stack(own_pieces, axis=1), jnp.stack(later_pieces, axis=1)], axis=0)
    partial = jnp.dot(
        pieces.reshape(2 * channels * stops, length),
        back_table,
        precision=lax.Precision.HIGHEST,
        preferred_element_type=jnp.float32,
    ).reshape(2, channels, stops, -1)
    summed = partial + swapped(partial, "rep")
    own_part, later_part = summed[0], summed[1]
    scale = 1.0 / math.sqrt(segments * lax.axis_size("rep") * half_len)
    correlations = []
    mirrored = []
    for stop in range(1, stops + 1):
        from_earlier = shifted(later_part[:, stop - 1], "blk", stop)
        from_later = shifted(own_part[:, stop - 1], "blk", -stop)
        correlations.append((own_part[:, stop - 1] + from_earlier) * scale)
        mirrored.append(((from_later + later_part[:, stop - 1]) * scale)[:, ::-1])
    return (jnp.stack(correlations, axis=1), jnp.stack(mirrored, axis=1))


def solution(mesh):
    return jax.shard_map(
        on_device,
        mesh=mesh,
        in_specs=(P("blk", "rep", None), P(None, "blk"), P("blk")),
        out_specs=(P("blk", None, None), P("blk", None, None)),
        check_vma=False,
    )
```

```python
import math

import jax
import jax.numpy as jnp
from jax import lax
from jax.sharding import PartitionSpec as P

LAGS = 128


def shifted(x, axis, by):
    length = lax.axis_size(axis)
    return lax.ppermute(x, axis, [(i, (i + by) % length) for i in range(length)])


def swapped(x, axis):
    length = lax.axis_size(axis)
    return lax.ppermute(x, axis, [(i, i ^ 1) for i in range(length)])


def cos_sin(phase, length):
    angle = phase.astype(jnp.float32) * (2.0 * math.pi / length)
    return jnp.cos(angle), jnp.sin(angle)


def forward_table(length):
    half_len = length // 2
    lo_len = 64
    hi_len = length // lo_len
    bin_idx = lax.iota(jnp.int32, half_len)
    hi_idx = lax.iota(jnp.int32, hi_len) * lo_len
    lo_idx = lax.iota(jnp.int32, lo_len)
    cos_hi, sin_hi = cos_sin(hi_idx[:, None] * bin_idx[None, :] % length, length)
    cos_lo, sin_lo = cos_sin(lo_idx[:, None] * bin_idx[None, :] % length, length)
    cos_hi, sin_hi = cos_hi[:, None, :], sin_hi[:, None, :]
    cos_lo, sin_lo = cos_lo[None, :, :], sin_lo[None, :, :]
    cos_t = cos_hi * cos_lo - sin_hi * sin_lo
    sin_t = sin_hi * cos_lo + cos_hi * sin_lo
    table = jnp.concatenate([cos_t, -sin_t], axis=-1)
    return table.reshape(length, length).astype(jnp.bfloat16)


def inverse_table(length, lag_half):
    half_len = length // 2
    lo_len = 32
    hi_len = half_len // lo_len
    lag_idx = (lax.iota(jnp.int32, 2 * lag_half + 1) - lag_half) % length
    hi_idx = lax.iota(jnp.int32, hi_len) * lo_len
    lo_idx = lax.iota(jnp.int32, lo_len)
    cos_hi, sin_hi = cos_sin(hi_idx[:, None] * lag_idx[None, :] % length, length)
    cos_lo, sin_lo = cos_sin(lo_idx[:, None] * lag_idx[None, :] % length, length)
    cos_hi, sin_hi = cos_hi[:, None, :], sin_hi[:, None, :]
    cos_lo, sin_lo = cos_lo[None, :, :], sin_lo[None, :, :]
    cos_t = (cos_hi * cos_lo - sin_hi * sin_lo).reshape(half_len, -1)
    sin_t = (sin_hi * cos_lo + cos_hi * sin_lo).reshape(half_len, -1)
    return jnp.concatenate([cos_t, -sin_t], axis=0)


def whiten(spectrum, keep, half_len):
    power = jnp.sum(spectrum * spectrum, axis=-1, keepdims=True) / half_len
    return (spectrum * lax.rsqrt(power + 1e-06) * keep[:, None, None]).astype(jnp.bfloat16)


def cross_spectrum(local, partner, half_len):
    first = local.astype(jnp.float32)
    second = partner.astype(jnp.float32)
    real_a, imag_a = (first[..., :half_len], first[..., half_len:])
    real_b, imag_b = (second[..., :half_len], second[..., half_len:])
    real_sum = jnp.sum(real_a * real_b + imag_a * imag_b, axis=1)
    imag_sum = jnp.sum(imag_a * real_b - real_a * imag_b, axis=1)
    return jnp.concatenate([real_sum, imag_sum], axis=-1)


def on_device(samples, offsets, bad_mask):
    channels, segments, length = samples.shape
    half_len = length // 2
    stops = offsets.shape[0]
    spectrum = jnp.dot(
        samples.reshape(channels * segments, length),
        forward_table(length),
        preferred_element_type=jnp.float32,
    ).reshape(channels, segments, length)
    keep = (1 - bad_mask).astype(jnp.float32)
    white = whiten(spectrum, keep, half_len)
    split = segments // 2
    ahead = white[:, :split]
    behind = white[:, split:]
    dc_imag = lax.broadcasted_iota(jnp.int32, behind.shape, 2) == half_len
    moving_ahead = ahead
    moving_behind = behind.at[:, :stops, half_len].set(offsets.T.astype(jnp.bfloat16))
    own_pieces = []
    later_pieces = []
    for stop in range(1, stops + 1):
        moving_ahead, moving_behind = lax.optimization_barrier(
            (shifted(moving_ahead, "blk", 1), shifted(moving_behind, "blk", -1))
        )
        partner = jnp.take(moving_ahead, offsets[stop - 1], axis=0)
        own_pieces.append(cross_spectrum(ahead, partner, half_len))
        later_offsets = moving_behind[:, stop - 1, half_len].astype(jnp.int32)
        local_partner = jnp.take(behind, later_offsets, axis=0)
        later = jnp.where(dc_imag, jnp.zeros_like(moving_behind), moving_behind)
        later_pieces.append(cross_spectrum(later, local_partner, half_len))
    back_table = inverse_table(length, LAGS)
    pieces = jnp.stack([jnp.stack(own_pieces, axis=1), jnp.stack(later_pieces, axis=1)], axis=0)
    partial = jnp.dot(
        pieces.reshape(2 * channels * stops, length),
        back_table,
        precision=lax.Precision.HIGHEST,
        preferred_element_type=jnp.float32,
    ).reshape(2, channels, stops, -1)
    summed = partial + swapped(partial, "rep")
    own_part, later_part = summed[0], summed[1]
    scale = 1.0 / math.sqrt(segments * lax.axis_size("rep") * half_len)
    correlations = []
    mirrored = []
    for stop in range(1, stops + 1):
        from_earlier = shifted(later_part[:, stop - 1], "blk", stop)
        from_later = shifted(own_part[:, stop - 1], "blk", -stop)
        correlations.append((own_part[:, stop - 1] + from_earlier) * scale)
        mirrored.append(((from_later + later_part[:, stop - 1]) * scale)[:, ::-1])
    return (jnp.stack(correlations, axis=1), jnp.stack(mirrored, axis=1))


def solution(mesh):
    return jax.shard_map(
        on_device,
        mesh=mesh,
        in_specs=(P("blk", "rep", None), P(None, "blk"), P("blk")),
        out_specs=(P("blk", None, None), P("blk", None, None)),
        check_vma=False,
    )
```

```python
import math

import jax
import jax.numpy as jnp
from jax import lax
from jax.sharding import PartitionSpec as P

LAGS = 128


def shifted(x, axis, by):
    length = lax.axis_size(axis)
    return lax.ppermute(x, axis, [(i, (i + by) % length) for i in range(length)])


def swapped(x, axis):
    length = lax.axis_size(axis)
    return lax.ppermute(x, axis, [(i, i ^ 1) for i in range(length)])


def cos_sin(phase, length):
    angle = phase.astype(jnp.float32) * (2.0 * math.pi / length)
    return jnp.cos(angle), jnp.sin(angle)


def forward_table(length):
    half_len = length // 2
    lo_len = 64
    hi_len = length // lo_len
    bin_idx = lax.iota(jnp.int32, half_len)
    hi_idx = lax.iota(jnp.int32, hi_len) * lo_len
    lo_idx = lax.iota(jnp.int32, lo_len)
    cos_hi, sin_hi = cos_sin(hi_idx[:, None] * bin_idx[None, :] % length, length)
    cos_lo, sin_lo = cos_sin(lo_idx[:, None] * bin_idx[None, :] % length, length)
    cos_hi, sin_hi = cos_hi[:, None, :], sin_hi[:, None, :]
    cos_lo, sin_lo = cos_lo[None, :, :], sin_lo[None, :, :]
    cos_t = cos_hi * cos_lo - sin_hi * sin_lo
    sin_t = sin_hi * cos_lo + cos_hi * sin_lo
    table = jnp.concatenate([cos_t, -sin_t], axis=-1)
    return table.reshape(length, length).astype(jnp.bfloat16)


def inverse_table(length, lag_half):
    half_len = length // 2
    lo_len = 32
    hi_len = half_len // lo_len
    lag_idx = (lax.iota(jnp.int32, 2 * lag_half + 1) - lag_half) % length
    hi_idx = lax.iota(jnp.int32, hi_len) * lo_len
    lo_idx = lax.iota(jnp.int32, lo_len)
    cos_hi, sin_hi = cos_sin(hi_idx[:, None] * lag_idx[None, :] % length, length)
    cos_lo, sin_lo = cos_sin(lo_idx[:, None] * lag_idx[None, :] % length, length)
    cos_hi, sin_hi = cos_hi[:, None, :], sin_hi[:, None, :]
    cos_lo, sin_lo = cos_lo[None, :, :], sin_lo[None, :, :]
    cos_t = (cos_hi * cos_lo - sin_hi * sin_lo).reshape(half_len, -1)
    sin_t = (sin_hi * cos_lo + cos_hi * sin_lo).reshape(half_len, -1)
    return jnp.concatenate([cos_t, -sin_t], axis=0)


def whiten(spectrum, keep, half_len):
    power = jnp.sum(spectrum * spectrum, axis=-1, keepdims=True) / half_len
    return (spectrum * lax.rsqrt(power + 1e-06) * keep[:, None, None]).astype(jnp.bfloat16)


def cross_spectrum(local, partner, half_len):
    first = local.astype(jnp.float32)
    second = partner.astype(jnp.float32)
    real_a, imag_a = (first[..., :half_len], first[..., half_len:])
    real_b, imag_b = (second[..., :half_len], second[..., half_len:])
    real_sum = jnp.sum(real_a * real_b + imag_a * imag_b, axis=1)
    imag_sum = jnp.sum(imag_a * real_b - real_a * imag_b, axis=1)
    return jnp.concatenate([real_sum, imag_sum], axis=-1)


def on_device(samples, offsets, bad_mask):
    channels, segments, length = samples.shape
    half_len = length // 2
    stops = offsets.shape[0]
    spectrum = jnp.dot(
        samples.reshape(channels * segments, length),
        forward_table(length),
        preferred_element_type=jnp.float32,
    ).reshape(channels, segments, length)
    keep = (1 - bad_mask).astype(jnp.float32)
    white = whiten(spectrum, keep, half_len)
    split = segments // 2
    ahead = white[:, :split]
    behind = white[:, split:]
    dc_imag = lax.broadcasted_iota(jnp.int32, behind.shape, 2) == half_len
    moving_ahead = ahead
    moving_behind = behind.at[:, :stops, half_len].set(offsets.T.astype(jnp.bfloat16))
    back_table = inverse_table(length, LAGS)
    own_parts, later_parts, from_earlier, from_later = [], [], [], []
    lags = jnp.zeros((2 * channels, back_table.shape[1]), jnp.float32)
    for stop in range(1, stops + 1):
        moving_ahead, moving_behind, lags = lax.optimization_barrier(
            (shifted(moving_ahead, "blk", 1), shifted(moving_behind, "blk", -1), lags)
        )
        if stop > 1:
            own_parts.append(lags[:channels])
            later_parts.append(lags[channels:])
            from_earlier.append(shifted(lags[channels:], "blk", stop - 1))
            from_later.append(shifted(lags[:channels], "blk", 1 - stop))
        partner = jnp.take(moving_ahead, offsets[stop - 1], axis=0)
        own = cross_spectrum(ahead, partner, half_len)
        later_offsets = moving_behind[:, stop - 1, half_len].astype(jnp.int32)
        local_partner = jnp.take(behind, later_offsets, axis=0)
        later = jnp.where(dc_imag, jnp.zeros_like(moving_behind), moving_behind)
        later = cross_spectrum(later, local_partner, half_len)
        lags = jnp.dot(
            jnp.concatenate([own, later], axis=0),
            back_table,
            precision=lax.Precision.HIGHEST,
            preferred_element_type=jnp.float32,
        )
    own_parts.append(lags[:channels])
    later_parts.append(lags[channels:])
    from_earlier.append(shifted(lags[channels:], "blk", stops))
    from_later.append(shifted(lags[:channels], "blk", -stops))
    corr_part = jnp.stack(own_parts, axis=1) + jnp.stack(from_earlier, axis=1)
    mirror_part = jnp.stack(from_later, axis=1) + jnp.stack(later_parts, axis=1)
    parts = jnp.stack([corr_part, mirror_part], axis=0)
    summed = parts + swapped(parts, "rep")
    scale = 1.0 / math.sqrt(segments * lax.axis_size("rep") * half_len)
    correlations = summed[0] * scale
    mirrored = (summed[1] * scale)[:, :, ::-1]
    return (correlations, mirrored)


def solution(mesh):
    return jax.shard_map(
        on_device,
        mesh=mesh,
        in_specs=(P("blk", "rep", None), P(None, "blk"), P("blk")),
        out_specs=(P("blk", None, None), P("blk", None, None)),
        check_vma=False,
    )
```

```python
import math

import jax
import jax.numpy as jnp
from jax import lax
from jax.sharding import PartitionSpec as P

LAGS = 128


def shifted(x, axis, by):
    length = lax.axis_size(axis)
    return lax.ppermute(x, axis, [(i, (i + by) % length) for i in range(length)])


def swapped(x, axis):
    length = lax.axis_size(axis)
    return lax.ppermute(x, axis, [(i, i ^ 1) for i in range(length)])


def cos_sin(phase, length):
    angle = phase.astype(jnp.float32) * (2.0 * math.pi / length)
    return jnp.cos(angle), jnp.sin(angle)


def forward_table(length):
    half_len = length // 2
    lo_len = 64
    hi_len = length // lo_len
    bin_idx = lax.iota(jnp.int32, half_len)
    hi_idx = lax.iota(jnp.int32, hi_len) * lo_len
    lo_idx = lax.iota(jnp.int32, lo_len)
    cos_hi, sin_hi = cos_sin(hi_idx[:, None] * bin_idx[None, :] % length, length)
    cos_lo, sin_lo = cos_sin(lo_idx[:, None] * bin_idx[None, :] % length, length)
    cos_hi, sin_hi = cos_hi[:, None, :], sin_hi[:, None, :]
    cos_lo, sin_lo = cos_lo[None, :, :], sin_lo[None, :, :]
    cos_t = cos_hi * cos_lo - sin_hi * sin_lo
    sin_t = sin_hi * cos_lo + cos_hi * sin_lo
    table = jnp.concatenate([cos_t, -sin_t], axis=-1)
    return table.reshape(length, length).astype(jnp.bfloat16)


def inverse_table(length, lag_half):
    half_len = length // 2
    lo_len = 32
    hi_len = half_len // lo_len
    lag_idx = (lax.iota(jnp.int32, 2 * lag_half + 1) - lag_half) % length
    hi_idx = lax.iota(jnp.int32, hi_len) * lo_len
    lo_idx = lax.iota(jnp.int32, lo_len)
    cos_hi, sin_hi = cos_sin(hi_idx[:, None] * lag_idx[None, :] % length, length)
    cos_lo, sin_lo = cos_sin(lo_idx[:, None] * lag_idx[None, :] % length, length)
    cos_hi, sin_hi = cos_hi[:, None, :], sin_hi[:, None, :]
    cos_lo, sin_lo = cos_lo[None, :, :], sin_lo[None, :, :]
    cos_t = (cos_hi * cos_lo - sin_hi * sin_lo).reshape(half_len, -1)
    sin_t = (sin_hi * cos_lo + cos_hi * sin_lo).reshape(half_len, -1)
    return jnp.concatenate([cos_t, -sin_t], axis=0)


def whiten(spectrum, keep, half_len):
    power = jnp.sum(spectrum * spectrum, axis=-1, keepdims=True) / half_len
    return (spectrum * lax.rsqrt(power + 1e-06) * keep).astype(jnp.bfloat16)


def cross_spectrum(local, partner, half_len):
    real_a, imag_a = (local[..., :half_len], local[..., half_len:])
    real_b, imag_b = (partner[..., :half_len], partner[..., half_len:])
    real_sum = jnp.sum(real_a * real_b + imag_a * imag_b, axis=0)
    imag_sum = jnp.sum(imag_a * real_b - real_a * imag_b, axis=0)
    return jnp.concatenate([real_sum, imag_sum], axis=-1)


def pick_rows(rows, block):
    picks = (rows[:, None] == lax.iota(jnp.int32, block.shape[1])[None, :]).astype(block.dtype)
    return jnp.einsum("gp,spk->sgk", picks, block, preferred_element_type=jnp.float32)


def on_device(samples, offsets, bad_mask):
    channels, segments, length = samples.shape
    half_len = length // 2
    stops = offsets.shape[0]
    spectrum = jnp.dot(
        jnp.swapaxes(samples, 0, 1).reshape(segments * channels, length),
        forward_table(length),
        preferred_element_type=jnp.float32,
    ).reshape(segments, channels, length)
    keep = (1 - bad_mask).astype(jnp.float32)
    white = whiten(spectrum, keep[None, :, None], half_len)
    split = segments // 2
    ahead = white[:split]
    behind = white[split:]
    ahead_f32 = ahead.astype(jnp.float32)
    dc_imag = lax.broadcasted_iota(jnp.int32, behind.shape, 2) == half_len
    moving_ahead = ahead
    moving_behind = behind.at[:stops, :, half_len].set(offsets.astype(jnp.bfloat16))
    back_table = inverse_table(length, LAGS)
    own_parts, later_parts, from_earlier, from_later = [], [], [], []
    lags = jnp.zeros((2 * channels, back_table.shape[1]), jnp.float32)
    for stop in range(1, stops + 1):
        moving_ahead, moving_behind, lags = lax.optimization_barrier(
            (shifted(moving_ahead, "blk", 1), shifted(moving_behind, "blk", -1), lags)
        )
        if stop > 1:
            own_parts.append(lags[:channels])
            later_parts.append(lags[channels:])
            from_earlier.append(shifted(lags[channels:], "blk", stop - 1))
            from_later.append(shifted(lags[:channels], "blk", 1 - stop))
        own = cross_spectrum(ahead_f32, pick_rows(offsets[stop - 1], moving_ahead), half_len)
        later_offsets = moving_behind[stop - 1, :, half_len].astype(jnp.int32)
        later = jnp.where(dc_imag, jnp.zeros_like(moving_behind), moving_behind).astype(jnp.float32)
        later = cross_spectrum(later, pick_rows(later_offsets, behind), half_len)
        lags = jnp.dot(
            jnp.concatenate([own, later], axis=0),
            back_table,
            precision=lax.Precision.HIGHEST,
            preferred_element_type=jnp.float32,
        )
    own_parts.append(lags[:channels])
    later_parts.append(lags[channels:])
    from_earlier.append(shifted(lags[channels:], "blk", stops))
    from_later.append(shifted(lags[:channels], "blk", -stops))
    corr_part = jnp.stack(own_parts, axis=1) + jnp.stack(from_earlier, axis=1)
    mirror_part = jnp.stack(from_later, axis=1) + jnp.stack(later_parts, axis=1)
    parts = jnp.stack([corr_part, mirror_part], axis=0)
    summed = parts + swapped(parts, "rep")
    scale = 1.0 / math.sqrt(segments * lax.axis_size("rep") * half_len)
    correlations = summed[0] * scale
    mirrored = (summed[1] * scale)[:, :, ::-1]
    return (correlations, mirrored)


def solution(mesh):
    return jax.shard_map(
        on_device,
        mesh=mesh,
        in_specs=(P("blk", "rep", None), P(None, "blk"), P("blk")),
        out_specs=(P("blk", None, None), P("blk", None, None)),
        check_vma=False,
    )
```

```python
import math

import jax
import jax.numpy as jnp
from jax import lax
from jax.sharding import PartitionSpec as P

LAGS = 128


def shifted(x, axis, by):
    length = lax.axis_size(axis)
    return lax.ppermute(x, axis, [(i, (i + by) % length) for i in range(length)])


def swapped(x, axis):
    length = lax.axis_size(axis)
    return lax.ppermute(x, axis, [(i, i ^ 1) for i in range(length)])


def cos_sin(phase, length):
    angle = phase.astype(jnp.float32) * (2.0 * math.pi / length)
    return jnp.cos(angle), jnp.sin(angle)


def forward_table(length):
    half_len = length // 2
    lo_len = 64
    hi_len = length // lo_len
    bin_idx = lax.iota(jnp.int32, half_len)
    hi_idx = lax.iota(jnp.int32, hi_len) * lo_len
    lo_idx = lax.iota(jnp.int32, lo_len)
    cos_hi, sin_hi = cos_sin(hi_idx[:, None] * bin_idx[None, :] % length, length)
    cos_lo, sin_lo = cos_sin(lo_idx[:, None] * bin_idx[None, :] % length, length)
    cos_hi, sin_hi = cos_hi[:, None, :], sin_hi[:, None, :]
    cos_lo, sin_lo = cos_lo[None, :, :], sin_lo[None, :, :]
    cos_t = cos_hi * cos_lo - sin_hi * sin_lo
    sin_t = sin_hi * cos_lo + cos_hi * sin_lo
    table = jnp.concatenate([cos_t, -sin_t], axis=-1)
    return table.reshape(length, length).astype(jnp.bfloat16)


def inverse_table(length, lag_half):
    half_len = length // 2
    lo_len = 32
    hi_len = half_len // lo_len
    lag_idx = (lax.iota(jnp.int32, 2 * lag_half + 1) - lag_half) % length
    hi_idx = lax.iota(jnp.int32, hi_len) * lo_len
    lo_idx = lax.iota(jnp.int32, lo_len)
    cos_hi, sin_hi = cos_sin(hi_idx[:, None] * lag_idx[None, :] % length, length)
    cos_lo, sin_lo = cos_sin(lo_idx[:, None] * lag_idx[None, :] % length, length)
    cos_hi, sin_hi = cos_hi[:, None, :], sin_hi[:, None, :]
    cos_lo, sin_lo = cos_lo[None, :, :], sin_lo[None, :, :]
    cos_t = (cos_hi * cos_lo - sin_hi * sin_lo).reshape(half_len, -1)
    sin_t = (sin_hi * cos_lo + cos_hi * sin_lo).reshape(half_len, -1)
    return jnp.concatenate([cos_t, -sin_t], axis=0)


def whiten(spectrum, keep, half_len):
    power = jnp.sum(spectrum * spectrum, axis=-1, keepdims=True) / half_len
    return (spectrum * lax.rsqrt(power + 1e-06) * keep).astype(jnp.bfloat16)


def cross_spectrum(local, partner, half_len):
    real_a, imag_a = (local[..., :half_len], local[..., half_len:])
    real_b, imag_b = (partner[..., :half_len], partner[..., half_len:])
    real_sum = jnp.sum(real_a * real_b + imag_a * imag_b, axis=0)
    imag_sum = jnp.sum(imag_a * real_b - real_a * imag_b, axis=0)
    return jnp.concatenate([real_sum, imag_sum], axis=-1)


def pick_rows(rows, block):
    picks = (rows[:, None] == lax.iota(jnp.int32, block.shape[1])[None, :]).astype(block.dtype)
    return jnp.einsum("gp,spk->sgk", picks, block, preferred_element_type=jnp.float32)


def on_device(samples, offsets, bad_mask):
    channels, segments, length = samples.shape
    half_len = length // 2
    stops = offsets.shape[0]
    spectrum = jnp.dot(
        jnp.swapaxes(samples, 0, 1).reshape(segments * channels, length),
        forward_table(length),
        preferred_element_type=jnp.float32,
    ).reshape(segments, channels, length)
    keep = (1 - bad_mask).astype(jnp.float32)
    white = whiten(spectrum, keep[None, :, None], half_len)
    split = segments // 2
    ahead = white[:split]
    behind = white[split:]
    ahead_f32 = ahead.astype(jnp.float32)
    dc_imag = lax.broadcasted_iota(jnp.int32, behind.shape, 2) == half_len
    moving_ahead = ahead
    moving_behind = behind.at[:stops, :, half_len].set(offsets.astype(jnp.bfloat16))
    back_table = inverse_table(length, LAGS)
    own_parts, later_parts, arrived = [], [], []
    lags = jnp.zeros((2 * channels, back_table.shape[1]), jnp.float32)
    in_flight = ()
    for stop in range(1, stops + 1):
        moving_ahead, moving_behind, lags, landed = lax.optimization_barrier(
            (shifted(moving_ahead, "blk", 1), shifted(moving_behind, "blk", -1), lags, in_flight)
        )
        arrived.extend(landed)
        in_flight = ()
        if stop > 1:
            own_parts.append(lags[:channels])
            later_parts.append(lags[channels:])
            in_flight = ((shifted(lags[channels:], "blk", stop - 1), shifted(lags[:channels], "blk", 1 - stop)),)
        own = cross_spectrum(ahead_f32, pick_rows(offsets[stop - 1], moving_ahead), half_len)
        later_offsets = moving_behind[stop - 1, :, half_len].astype(jnp.int32)
        later = jnp.where(dc_imag, jnp.zeros_like(moving_behind), moving_behind).astype(jnp.float32)
        later = cross_spectrum(later, pick_rows(later_offsets, behind), half_len)
        lags = jnp.dot(
            jnp.concatenate([own, later], axis=0),
            back_table,
            precision=lax.Precision.HIGHEST,
            preferred_element_type=jnp.float32,
        )
    arrived.extend(in_flight)
    own_parts.append(lags[:channels])
    later_parts.append(lags[channels:])
    arrived.append((shifted(lags[channels:], "blk", stops), shifted(lags[:channels], "blk", -stops)))
    from_earlier = [pair[0] for pair in arrived]
    from_later = [pair[1] for pair in arrived]
    corr_part = jnp.stack(own_parts, axis=1) + jnp.stack(from_earlier, axis=1)
    mirror_part = jnp.stack(from_later, axis=1) + jnp.stack(later_parts, axis=1)
    parts = jnp.stack([corr_part, mirror_part], axis=0)
    summed = parts + swapped(parts, "rep")
    scale = 1.0 / math.sqrt(segments * lax.axis_size("rep") * half_len)
    correlations = summed[0] * scale
    mirrored = (summed[1] * scale)[:, :, ::-1]
    return (correlations, mirrored)


def solution(mesh):
    return jax.shard_map(
        on_device,
        mesh=mesh,
        in_specs=(P("blk", "rep", None), P(None, "blk"), P("blk")),
        out_specs=(P("blk", None, None), P("blk", None, None)),
        check_vma=False,
    )
```

```python
import math

import jax
import jax.numpy as jnp
from jax import lax
from jax.sharding import PartitionSpec as P

LAGS = 128


def shifted(x, axis, by):
    length = lax.axis_size(axis)
    return lax.ppermute(x, axis, [(i, (i + by) % length) for i in range(length)])


def swapped(x, axis):
    length = lax.axis_size(axis)
    return lax.ppermute(x, axis, [(i, i ^ 1) for i in range(length)])


def cos_sin(phase, length):
    angle = phase.astype(jnp.float32) * (2.0 * math.pi / length)
    return jnp.cos(angle), jnp.sin(angle)


def forward_table(length):
    half_len = length // 2
    lo_len = 64
    hi_len = length // lo_len
    bin_idx = lax.iota(jnp.int32, half_len)
    hi_idx = lax.iota(jnp.int32, hi_len) * lo_len
    lo_idx = lax.iota(jnp.int32, lo_len)
    cos_hi, sin_hi = cos_sin(hi_idx[:, None] * bin_idx[None, :] % length, length)
    cos_lo, sin_lo = cos_sin(lo_idx[:, None] * bin_idx[None, :] % length, length)
    cos_hi, sin_hi = cos_hi[:, None, :], sin_hi[:, None, :]
    cos_lo, sin_lo = cos_lo[None, :, :], sin_lo[None, :, :]
    cos_t = cos_hi * cos_lo - sin_hi * sin_lo
    sin_t = sin_hi * cos_lo + cos_hi * sin_lo
    table = jnp.concatenate([cos_t, -sin_t], axis=-1)
    return table.reshape(length, length).astype(jnp.bfloat16)


def inverse_table(length, lag_half):
    half_len = length // 2
    lo_len = 32
    hi_len = half_len // lo_len
    lag_idx = (lax.iota(jnp.int32, 2 * lag_half + 1) - lag_half) % length
    hi_idx = lax.iota(jnp.int32, hi_len) * lo_len
    lo_idx = lax.iota(jnp.int32, lo_len)
    cos_hi, sin_hi = cos_sin(hi_idx[:, None] * lag_idx[None, :] % length, length)
    cos_lo, sin_lo = cos_sin(lo_idx[:, None] * lag_idx[None, :] % length, length)
    cos_hi, sin_hi = cos_hi[:, None, :], sin_hi[:, None, :]
    cos_lo, sin_lo = cos_lo[None, :, :], sin_lo[None, :, :]
    cos_t = (cos_hi * cos_lo - sin_hi * sin_lo).reshape(half_len, -1)
    sin_t = (sin_hi * cos_lo + cos_hi * sin_lo).reshape(half_len, -1)
    return jnp.concatenate([cos_t, -sin_t], axis=0)


def whiten(spectrum, keep, half_len):
    power = jnp.sum(spectrum * spectrum, axis=-1, keepdims=True) / half_len
    return (spectrum * lax.rsqrt(power + 1e-06) * keep).astype(jnp.bfloat16)


def cross_spectrum(local, partner, half_len):
    real_a, imag_a = (local[..., :half_len], local[..., half_len:])
    real_b, imag_b = (partner[..., :half_len], partner[..., half_len:])
    real_sum = jnp.sum(real_a * real_b + imag_a * imag_b, axis=0)
    imag_sum = jnp.sum(imag_a * real_b - real_a * imag_b, axis=0)
    return jnp.concatenate([real_sum, imag_sum], axis=-1)


def pick_rows(rows, block):
    picks = (rows[:, None] == lax.iota(jnp.int32, block.shape[1])[None, :]).astype(block.dtype)
    return jnp.einsum("gp,spk->sgk", picks, block, preferred_element_type=jnp.float32)


def on_device(samples, offsets, bad_mask):
    channels, segments, length = samples.shape
    half_len = length // 2
    stops = offsets.shape[0]
    spectrum = jnp.dot(
        jnp.swapaxes(samples, 0, 1).reshape(segments * channels, length),
        forward_table(length),
        preferred_element_type=jnp.float32,
    ).reshape(segments, channels, length)
    keep = (1 - bad_mask).astype(jnp.float32)
    white = whiten(spectrum, keep[None, :, None], half_len)
    split = segments // 2
    ahead = white[:split]
    behind = white[split:]
    ahead_f32 = ahead.astype(jnp.float32)
    dc_imag = lax.broadcasted_iota(jnp.int32, behind.shape, 2) == half_len
    moving_ahead = ahead
    moving_behind = behind.at[:stops, :, half_len].set(offsets.astype(jnp.bfloat16))
    back_table = inverse_table(length, LAGS)

    def lags_of(stop, earlier, later):
        own = cross_spectrum(ahead_f32, pick_rows(offsets[stop - 1], earlier), half_len)
        later_offsets = later[stop - 1, :, half_len].astype(jnp.int32)
        later = jnp.where(dc_imag, jnp.zeros_like(later), later).astype(jnp.float32)
        later = cross_spectrum(later, pick_rows(later_offsets, behind), half_len)
        return jnp.dot(
            jnp.concatenate([own, later], axis=0),
            back_table,
            precision=lax.Precision.HIGHEST,
            preferred_element_type=jnp.float32,
        )

    near = stops // 2
    first = lax.optimization_barrier(
        tuple(shifted(moving_ahead, "blk", d) for d in range(1, near + 1))
        + tuple(shifted(moving_behind, "blk", -d) for d in range(1, near + 1))
    )
    lags = [lags_of(d, first[d - 1], first[near + d - 1]) for d in range(1, near + 1)]
    far_ahead, far_behind, lags = lax.optimization_barrier(
        (
            shifted(jnp.concatenate(first[:near], axis=0), "blk", near),
            shifted(jnp.concatenate(first[near:], axis=0), "blk", -near),
            lags,
        )
    )
    for d in range(near + 1, stops + 1):
        at = (d - near - 1) * split
        lags.append(lags_of(d, far_ahead[at:at + split], far_behind[at:at + split]))
    own_parts = [piece[:channels] for piece in lags]
    later_parts = [piece[channels:] for piece in lags]
    from_earlier = [shifted(piece[channels:], "blk", d) for d, piece in enumerate(lags, 1)]
    from_later = [shifted(piece[:channels], "blk", -d) for d, piece in enumerate(lags, 1)]
    corr_part = jnp.stack(own_parts, axis=1) + jnp.stack(from_earlier, axis=1)
    mirror_part = jnp.stack(from_later, axis=1) + jnp.stack(later_parts, axis=1)
    parts = jnp.stack([corr_part, mirror_part], axis=0)
    summed = parts + swapped(parts, "rep")
    scale = 1.0 / math.sqrt(segments * lax.axis_size("rep") * half_len)
    correlations = summed[0] * scale
    mirrored = (summed[1] * scale)[:, :, ::-1]
    return (correlations, mirrored)


def solution(mesh):
    return jax.shard_map(
        on_device,
        mesh=mesh,
        in_specs=(P("blk", "rep", None), P(None, "blk"), P("blk")),
        out_specs=(P("blk", None, None), P("blk", None, None)),
        check_vma=False,
    )
```

```python
import math

import jax
import jax.numpy as jnp
from jax import lax
from jax.sharding import PartitionSpec as P

LAGS = 128


def shifted(x, axis, by):
    length = lax.axis_size(axis)
    return lax.ppermute(x, axis, [(i, (i + by) % length) for i in range(length)])


def swapped(x, axis):
    length = lax.axis_size(axis)
    return lax.ppermute(x, axis, [(i, i ^ 1) for i in range(length)])


def cos_sin(phase, length):
    angle = phase.astype(jnp.float32) * (2.0 * math.pi / length)
    return jnp.cos(angle), jnp.sin(angle)


def forward_table(length):
    half_len = length // 2
    lo_len = 64
    hi_len = length // lo_len
    bin_idx = lax.iota(jnp.int32, half_len)
    hi_idx = lax.iota(jnp.int32, hi_len) * lo_len
    lo_idx = lax.iota(jnp.int32, lo_len)
    cos_hi, sin_hi = cos_sin(hi_idx[:, None] * bin_idx[None, :] % length, length)
    cos_lo, sin_lo = cos_sin(lo_idx[:, None] * bin_idx[None, :] % length, length)
    cos_hi, sin_hi = cos_hi[:, None, :], sin_hi[:, None, :]
    cos_lo, sin_lo = cos_lo[None, :, :], sin_lo[None, :, :]
    cos_t = cos_hi * cos_lo - sin_hi * sin_lo
    sin_t = sin_hi * cos_lo + cos_hi * sin_lo
    table = jnp.concatenate([cos_t, -sin_t], axis=-1)
    return table.reshape(length, length).astype(jnp.bfloat16)


def inverse_table(length, lag_half):
    half_len = length // 2
    lo_len = 32
    hi_len = half_len // lo_len
    lag_idx = (lax.iota(jnp.int32, 2 * lag_half + 1) - lag_half) % length
    hi_idx = lax.iota(jnp.int32, hi_len) * lo_len
    lo_idx = lax.iota(jnp.int32, lo_len)
    cos_hi, sin_hi = cos_sin(hi_idx[:, None] * lag_idx[None, :] % length, length)
    cos_lo, sin_lo = cos_sin(lo_idx[:, None] * lag_idx[None, :] % length, length)
    cos_hi, sin_hi = cos_hi[:, None, :], sin_hi[:, None, :]
    cos_lo, sin_lo = cos_lo[None, :, :], sin_lo[None, :, :]
    cos_t = (cos_hi * cos_lo - sin_hi * sin_lo).reshape(half_len, -1)
    sin_t = (sin_hi * cos_lo + cos_hi * sin_lo).reshape(half_len, -1)
    return jnp.concatenate([cos_t, -sin_t], axis=0)


def whiten(spectrum, keep, half_len):
    power = jnp.sum(spectrum * spectrum, axis=-1, keepdims=True) / half_len
    return (spectrum * lax.rsqrt(power + 1e-06) * keep).astype(jnp.bfloat16)


def cross_spectrum(local, partner, half_len):
    real_a, imag_a = (local[..., :half_len], local[..., half_len:])
    real_b, imag_b = (partner[..., :half_len], partner[..., half_len:])
    real_sum = jnp.sum(real_a * real_b + imag_a * imag_b, axis=0)
    imag_sum = jnp.sum(imag_a * real_b - real_a * imag_b, axis=0)
    return jnp.concatenate([real_sum, imag_sum], axis=-1)


def pick_rows(rows, block):
    picks = (rows[:, None] == lax.iota(jnp.int32, block.shape[1])[None, :]).astype(block.dtype)
    return jnp.einsum("gp,spk->sgk", picks, block, preferred_element_type=jnp.float32)


def on_device(samples, offsets, bad_mask):
    channels, segments, length = samples.shape
    half_len = length // 2
    stops = offsets.shape[0]
    spectrum = jnp.dot(
        jnp.swapaxes(samples, 0, 1).reshape(segments * channels, length),
        forward_table(length),
        preferred_element_type=jnp.float32,
    ).reshape(segments, channels, length)
    keep = (1 - bad_mask).astype(jnp.float32)
    white = whiten(spectrum, keep[None, :, None], half_len)
    split = segments // 2
    ahead = white[:split]
    behind = white[split:]
    ahead_f32 = ahead.astype(jnp.float32)
    dc_imag = lax.broadcasted_iota(jnp.int32, behind.shape, 2) == half_len
    moving_ahead = ahead
    moving_behind = behind.at[:stops, :, half_len].set(offsets.astype(jnp.bfloat16))
    back_table = inverse_table(length, LAGS)

    def lags_of(stop, earlier, later):
        own = cross_spectrum(ahead_f32, pick_rows(offsets[stop - 1], earlier), half_len)
        later_offsets = later[stop - 1, :, half_len].astype(jnp.int32)
        later = jnp.where(dc_imag, jnp.zeros_like(later), later).astype(jnp.float32)
        later = cross_spectrum(later, pick_rows(later_offsets, behind), half_len)
        return jnp.dot(
            jnp.concatenate([own, later], axis=0),
            back_table,
            precision=lax.Precision.HIGHEST,
            preferred_element_type=jnp.float32,
        )

    near = stops // 2
    first = lax.optimization_barrier(
        tuple(shifted(moving_ahead, "blk", d) for d in range(1, near + 1))
        + tuple(shifted(moving_behind, "blk", -d) for d in range(1, near + 1))
    )
    lags = [lags_of(d, first[d - 1], first[near + d - 1]) for d in range(1, near + 1)]
    early = [
        (shifted(piece[channels:], "blk", d), shifted(piece[:channels], "blk", -d)) for d, piece in enumerate(lags, 1)
    ]
    far_ahead, far_behind, early = lax.optimization_barrier(
        (
            shifted(jnp.concatenate(first[:near], axis=0), "blk", near),
            shifted(jnp.concatenate(first[near:], axis=0), "blk", -near),
            early,
        )
    )
    for d in range(near + 1, stops + 1):
        at = (d - near - 1) * split
        lags.append(lags_of(d, far_ahead[at:at + split], far_behind[at:at + split]))
    late = [(shifted(lags[d - 1][channels:], "blk", d), shifted(lags[d - 1][:channels], "blk", -d)) for d in
            range(near + 1, stops + 1)]
    own_parts = [piece[:channels] for piece in lags]
    later_parts = [piece[channels:] for piece in lags]
    from_earlier = [pair[0] for pair in early + late]
    from_later = [pair[1] for pair in early + late]
    corr_part = jnp.stack(own_parts, axis=1) + jnp.stack(from_earlier, axis=1)
    mirror_part = jnp.stack(from_later, axis=1) + jnp.stack(later_parts, axis=1)
    parts = jnp.stack([corr_part, mirror_part], axis=0)
    summed = parts + swapped(parts, "rep")
    scale = 1.0 / math.sqrt(segments * lax.axis_size("rep") * half_len)
    correlations = summed[0] * scale
    mirrored = (summed[1] * scale)[:, :, ::-1]
    return (correlations, mirrored)


def solution(mesh):
    return jax.shard_map(
        on_device,
        mesh=mesh,
        in_specs=(P("blk", "rep", None), P(None, "blk"), P("blk")),
        out_specs=(P("blk", None, None), P("blk", None, None)),
        check_vma=False,
    )
```

```python
import math

import jax
import jax.numpy as jnp
from jax import lax
from jax.sharding import PartitionSpec as P

LAGS = 128


def shifted(x, axis, by):
    length = lax.axis_size(axis)
    return lax.ppermute(x, axis, [(i, (i + by) % length) for i in range(length)])


def swapped(x, axis):
    length = lax.axis_size(axis)
    return lax.ppermute(x, axis, [(i, i ^ 1) for i in range(length)])


def cos_sin(phase, length):
    angle = phase.astype(jnp.float32) * (2.0 * math.pi / length)
    return jnp.cos(angle), jnp.sin(angle)


def forward_table(length):
    half_len = length // 2
    lo_len = 64
    hi_len = length // lo_len
    bin_idx = lax.iota(jnp.int32, half_len)
    hi_idx = lax.iota(jnp.int32, hi_len) * lo_len
    lo_idx = lax.iota(jnp.int32, lo_len)
    cos_hi, sin_hi = cos_sin(hi_idx[:, None] * bin_idx[None, :] % length, length)
    cos_lo, sin_lo = cos_sin(lo_idx[:, None] * bin_idx[None, :] % length, length)
    cos_hi, sin_hi = cos_hi[:, None, :], sin_hi[:, None, :]
    cos_lo, sin_lo = cos_lo[None, :, :], sin_lo[None, :, :]
    cos_t = cos_hi * cos_lo - sin_hi * sin_lo
    sin_t = sin_hi * cos_lo + cos_hi * sin_lo
    table = jnp.concatenate([cos_t, -sin_t], axis=-1)
    return table.reshape(length, length).astype(jnp.bfloat16)


def inverse_table(length, lag_half):
    half_len = length // 2
    lo_len = 32
    hi_len = half_len // lo_len
    lag_idx = (lax.iota(jnp.int32, 2 * lag_half + 1) - lag_half) % length
    hi_idx = lax.iota(jnp.int32, hi_len) * lo_len
    lo_idx = lax.iota(jnp.int32, lo_len)
    cos_hi, sin_hi = cos_sin(hi_idx[:, None] * lag_idx[None, :] % length, length)
    cos_lo, sin_lo = cos_sin(lo_idx[:, None] * lag_idx[None, :] % length, length)
    cos_hi, sin_hi = cos_hi[:, None, :], sin_hi[:, None, :]
    cos_lo, sin_lo = cos_lo[None, :, :], sin_lo[None, :, :]
    cos_t = (cos_hi * cos_lo - sin_hi * sin_lo).reshape(half_len, -1)
    sin_t = (sin_hi * cos_lo + cos_hi * sin_lo).reshape(half_len, -1)
    return jnp.concatenate([cos_t, -sin_t], axis=0)


def whiten(spectrum, keep, half_len):
    power = jnp.sum(spectrum * spectrum, axis=-1, keepdims=True) / half_len
    return (spectrum * lax.rsqrt(power + 1e-06) * keep).astype(jnp.bfloat16)


def cross_spectrum(local, partner, half_len):
    real_a, imag_a = (local[..., :half_len], local[..., half_len:])
    real_b, imag_b = (partner[..., :half_len], partner[..., half_len:])
    real_sum = jnp.sum(real_a * real_b + imag_a * imag_b, axis=0)
    imag_sum = jnp.sum(imag_a * real_b - real_a * imag_b, axis=0)
    return jnp.concatenate([real_sum, imag_sum], axis=-1)


def pick_rows(rows, block):
    picks = (rows[:, None] == lax.iota(jnp.int32, block.shape[1])[None, :]).astype(block.dtype)
    return jnp.einsum("gp,spk->sgk", picks, block, preferred_element_type=jnp.float32)


def on_device(samples, offsets, bad_mask):
    channels, segments, length = samples.shape
    half_len = length // 2
    stops = offsets.shape[0]
    spectrum = jnp.dot(
        jnp.swapaxes(samples, 0, 1).reshape(segments * channels, length),
        forward_table(length),
        preferred_element_type=jnp.float32,
    ).reshape(segments, channels, length)
    keep = (1 - bad_mask).astype(jnp.float32)
    white = whiten(spectrum, keep[None, :, None], half_len)
    split = segments // 2
    ahead = white[:split]
    behind = white[split:]
    ahead_f32 = ahead.astype(jnp.float32)
    dc_imag = lax.broadcasted_iota(jnp.int32, behind.shape, 2) == half_len
    moving_ahead = ahead
    moving_behind = behind.at[:stops, :, half_len].set(offsets.astype(jnp.bfloat16))
    back_table = inverse_table(length, LAGS)

    def lags_of(stop, earlier, later):
        own = cross_spectrum(ahead_f32, pick_rows(offsets[stop - 1], earlier), half_len)
        later_offsets = later[stop - 1, :, half_len].astype(jnp.int32)
        later = jnp.where(dc_imag, jnp.zeros_like(later), later).astype(jnp.float32)
        later = cross_spectrum(later, pick_rows(later_offsets, behind), half_len)
        return jnp.dot(
            jnp.concatenate([own, later], axis=0),
            back_table,
            precision=lax.Precision.HIGHEST,
            preferred_element_type=jnp.float32,
        )

    near = stops // 2
    first = lax.optimization_barrier(
        tuple(shifted(moving_ahead, "blk", d) for d in range(1, near + 1))
        + tuple(shifted(moving_behind, "blk", -d) for d in range(1, near + 1))
    )
    lags = [lags_of(d, first[d - 1], first[near + d - 1]) for d in range(1, near + 1)]
    early = [
        (shifted(piece[channels:], "blk", d), shifted(piece[:channels], "blk", -d)) for d, piece in enumerate(lags, 1)
    ]
    late = []
    for d in range(near + 1, stops + 1):
        far_ahead, far_behind, early = lax.optimization_barrier(
            (shifted(first[d - near - 1], "blk", near), shifted(first[d - 1], "blk", -near), early)
        )
        lags.append(lags_of(d, far_ahead, far_behind))
        late.append((shifted(lags[d - 1][channels:], "blk", d), shifted(lags[d - 1][:channels], "blk", -d)))
    own_parts = [piece[:channels] for piece in lags]
    later_parts = [piece[channels:] for piece in lags]
    from_earlier = [pair[0] for pair in early + late]
    from_later = [pair[1] for pair in early + late]
    corr_part = jnp.stack(own_parts, axis=1) + jnp.stack(from_earlier, axis=1)
    mirror_part = jnp.stack(from_later, axis=1) + jnp.stack(later_parts, axis=1)
    parts = jnp.stack([corr_part, mirror_part], axis=0)
    summed = parts + swapped(parts, "rep")
    scale = 1.0 / math.sqrt(segments * lax.axis_size("rep") * half_len)
    correlations = summed[0] * scale
    mirrored = (summed[1] * scale)[:, :, ::-1]
    return (correlations, mirrored)


def solution(mesh):
    return jax.shard_map(
        on_device,
        mesh=mesh,
        in_specs=(P("blk", "rep", None), P(None, "blk"), P("blk")),
        out_specs=(P("blk", None, None), P("blk", None, None)),
        check_vma=False,
    )
```

```python
import math

import jax
import jax.numpy as jnp
from jax import lax
from jax.sharding import PartitionSpec as P

LAGS = 128


def shifted(x, axis, by):
    length = lax.axis_size(axis)
    return lax.ppermute(x, axis, [(i, (i + by) % length) for i in range(length)])


def swapped(x, axis):
    length = lax.axis_size(axis)
    return lax.ppermute(x, axis, [(i, i ^ 1) for i in range(length)])


def cos_sin(phase, length):
    angle = phase.astype(jnp.float32) * (2.0 * math.pi / length)
    return jnp.cos(angle), jnp.sin(angle)


def forward_table(length):
    half_len = length // 2
    lo_len = 64
    hi_len = length // lo_len
    bin_idx = lax.iota(jnp.int32, half_len)
    hi_idx = lax.iota(jnp.int32, hi_len) * lo_len
    lo_idx = lax.iota(jnp.int32, lo_len)
    cos_hi, sin_hi = cos_sin(hi_idx[:, None] * bin_idx[None, :] % length, length)
    cos_lo, sin_lo = cos_sin(lo_idx[:, None] * bin_idx[None, :] % length, length)
    cos_hi, sin_hi = cos_hi[:, None, :], sin_hi[:, None, :]
    cos_lo, sin_lo = cos_lo[None, :, :], sin_lo[None, :, :]
    cos_t = cos_hi * cos_lo - sin_hi * sin_lo
    sin_t = sin_hi * cos_lo + cos_hi * sin_lo
    table = jnp.concatenate([cos_t, -sin_t], axis=-1)
    return table.reshape(length, length).astype(jnp.bfloat16)


def inverse_table(length, lag_half):
    half_len = length // 2
    lo_len = 32
    hi_len = half_len // lo_len
    lag_idx = (lax.iota(jnp.int32, 2 * lag_half + 1) - lag_half) % length
    hi_idx = lax.iota(jnp.int32, hi_len) * lo_len
    lo_idx = lax.iota(jnp.int32, lo_len)
    cos_hi, sin_hi = cos_sin(hi_idx[:, None] * lag_idx[None, :] % length, length)
    cos_lo, sin_lo = cos_sin(lo_idx[:, None] * lag_idx[None, :] % length, length)
    cos_hi, sin_hi = cos_hi[:, None, :], sin_hi[:, None, :]
    cos_lo, sin_lo = cos_lo[None, :, :], sin_lo[None, :, :]
    cos_t = (cos_hi * cos_lo - sin_hi * sin_lo).reshape(half_len, -1)
    sin_t = (sin_hi * cos_lo + cos_hi * sin_lo).reshape(half_len, -1)
    return jnp.concatenate([cos_t, -sin_t], axis=0)


def whiten(spectrum, keep, half_len):
    power = jnp.sum(spectrum * spectrum, axis=-1, keepdims=True) / half_len
    return (spectrum * lax.rsqrt(power + 1e-06) * keep).astype(jnp.bfloat16)


def cross_spectrum(local, partner, half_len):
    real_a, imag_a = (local[..., :half_len], local[..., half_len:])
    real_b, imag_b = (partner[..., :half_len], partner[..., half_len:])
    real_sum = jnp.sum(real_a * real_b + imag_a * imag_b, axis=0)
    imag_sum = jnp.sum(imag_a * real_b - real_a * imag_b, axis=0)
    return jnp.concatenate([real_sum, imag_sum], axis=-1)


def pick_rows(rows, block):
    picks = (rows[:, None] == lax.iota(jnp.int32, block.shape[1])[None, :]).astype(block.dtype)
    return jnp.einsum("gp,spk->sgk", picks, block, preferred_element_type=jnp.float32)


def on_device(samples, offsets, bad_mask):
    channels, segments, length = samples.shape
    half_len = length // 2
    stops = offsets.shape[0]
    spectrum = jnp.einsum("csn,nk->sck", samples, forward_table(length), preferred_element_type=jnp.float32)
    keep = (1 - bad_mask).astype(jnp.float32)
    white = whiten(spectrum, keep[None, :, None], half_len)
    split = segments // 2
    ahead = white[:split]
    behind = white[split:]
    ahead_f32 = ahead.astype(jnp.float32)
    dc_imag = lax.broadcasted_iota(jnp.int32, behind.shape, 2) == half_len
    moving_ahead = ahead
    moving_behind = behind.at[:stops, :, half_len].set(offsets.astype(jnp.bfloat16))
    back_table = inverse_table(length, LAGS)

    def lags_of(stop, earlier, later):
        own = cross_spectrum(ahead_f32, pick_rows(offsets[stop - 1], earlier), half_len)
        later_offsets = later[stop - 1, :, half_len].astype(jnp.int32)
        later = jnp.where(dc_imag, jnp.zeros_like(later), later).astype(jnp.float32)
        later = cross_spectrum(later, pick_rows(later_offsets, behind), half_len)
        return jnp.dot(
            jnp.concatenate([own, later], axis=0),
            back_table,
            precision=lax.Precision.HIGHEST,
            preferred_element_type=jnp.float32,
        )

    near = stops // 2
    first = lax.optimization_barrier(
        tuple(shifted(moving_ahead, "blk", d) for d in range(1, near + 1))
        + tuple(shifted(moving_behind, "blk", -d) for d in range(1, near + 1))
    )
    lags = [lags_of(d, first[d - 1], first[near + d - 1]) for d in range(1, near + 1)]
    early = [
        (shifted(piece[channels:], "blk", d), shifted(piece[:channels], "blk", -d)) for d, piece in enumerate(lags, 1)
    ]
    far_ahead, far_behind, early = lax.optimization_barrier(
        (
            shifted(jnp.concatenate(first[:near], axis=0), "blk", near),
            shifted(jnp.concatenate(first[near:], axis=0), "blk", -near),
            early,
        )
    )
    for d in range(near + 1, stops + 1):
        at = (d - near - 1) * split
        lags.append(lags_of(d, far_ahead[at:at + split], far_behind[at:at + split]))
    late = [(shifted(lags[d - 1][channels:], "blk", d), shifted(lags[d - 1][:channels], "blk", -d)) for d in
            range(near + 1, stops + 1)]
    own_parts = [piece[:channels] for piece in lags]
    later_parts = [piece[channels:] for piece in lags]
    from_earlier = [pair[0] for pair in early + late]
    from_later = [pair[1] for pair in early + late]
    corr_part = jnp.stack(own_parts, axis=1) + jnp.stack(from_earlier, axis=1)
    mirror_part = jnp.stack(from_later, axis=1) + jnp.stack(later_parts, axis=1)
    parts = jnp.stack([corr_part, mirror_part], axis=0)
    summed = parts + swapped(parts, "rep")
    scale = 1.0 / math.sqrt(segments * lax.axis_size("rep") * half_len)
    correlations = summed[0] * scale
    mirrored = (summed[1] * scale)[:, :, ::-1]
    return (correlations, mirrored)


def solution(mesh):
    return jax.shard_map(
        on_device,
        mesh=mesh,
        in_specs=(P("blk", "rep", None), P(None, "blk"), P("blk")),
        out_specs=(P("blk", None, None), P("blk", None, None)),
        check_vma=False,
    )
```

```python
import math

import jax
import jax.numpy as jnp
from jax import lax
from jax.sharding import PartitionSpec as P

LAGS = 128


def shifted(x, axis, by):
    length = lax.axis_size(axis)
    return lax.ppermute(x, axis, [(i, (i + by) % length) for i in range(length)])


def swapped(x, axis):
    length = lax.axis_size(axis)
    return lax.ppermute(x, axis, [(i, i ^ 1) for i in range(length)])


def along(x, first_by, second_by, flip=False):
    blocks = lax.axis_size("blk")
    land = 1 if flip else 0
    perm = [(b * 2, ((b + first_by) % blocks) * 2 + land) for b in range(blocks)]
    perm += [(b * 2 + 1, ((b + second_by) % blocks) * 2 + 1 - land) for b in range(blocks)]
    return lax.ppermute(x, ("blk", "rep"), perm)


def cos_sin(phase, length):
    angle = phase.astype(jnp.float32) * (2.0 * math.pi / length)
    return jnp.cos(angle), jnp.sin(angle)


def forward_table(length):
    half_len = length // 2
    lo_len = 64
    hi_len = length // lo_len
    bin_idx = lax.iota(jnp.int32, half_len)
    hi_idx = lax.iota(jnp.int32, hi_len) * lo_len
    lo_idx = lax.iota(jnp.int32, lo_len)
    cos_hi, sin_hi = cos_sin(hi_idx[:, None] * bin_idx[None, :] % length, length)
    cos_lo, sin_lo = cos_sin(lo_idx[:, None] * bin_idx[None, :] % length, length)
    cos_hi, sin_hi = cos_hi[:, None, :], sin_hi[:, None, :]
    cos_lo, sin_lo = cos_lo[None, :, :], sin_lo[None, :, :]
    cos_t = cos_hi * cos_lo - sin_hi * sin_lo
    sin_t = sin_hi * cos_lo + cos_hi * sin_lo
    table = jnp.concatenate([cos_t, -sin_t], axis=-1)
    return table.reshape(length, length).astype(jnp.bfloat16)


def inverse_table(length, lag_half):
    half_len = length // 2
    lo_len = 32
    hi_len = half_len // lo_len
    lag_idx = (lax.iota(jnp.int32, 2 * lag_half + 1) - lag_half) % length
    hi_idx = lax.iota(jnp.int32, hi_len) * lo_len
    lo_idx = lax.iota(jnp.int32, lo_len)
    cos_hi, sin_hi = cos_sin(hi_idx[:, None] * lag_idx[None, :] % length, length)
    cos_lo, sin_lo = cos_sin(lo_idx[:, None] * lag_idx[None, :] % length, length)
    cos_hi, sin_hi = cos_hi[:, None, :], sin_hi[:, None, :]
    cos_lo, sin_lo = cos_lo[None, :, :], sin_lo[None, :, :]
    cos_t = (cos_hi * cos_lo - sin_hi * sin_lo).reshape(half_len, -1)
    sin_t = (sin_hi * cos_lo + cos_hi * sin_lo).reshape(half_len, -1)
    return jnp.concatenate([cos_t, -sin_t], axis=0)


def whiten(spectrum, keep, half_len):
    power = jnp.sum(spectrum * spectrum, axis=-1, keepdims=True) / half_len
    return (spectrum * lax.rsqrt(power + 1e-06) * keep).astype(jnp.bfloat16)


def cross_spectrum(local, partner, half_len):
    real_a, imag_a = (local[..., :half_len], local[..., half_len:])
    real_b, imag_b = (partner[..., :half_len], partner[..., half_len:])
    real_sum = jnp.sum(real_a * real_b + imag_a * imag_b, axis=0)
    imag_sum = jnp.sum(imag_a * real_b - real_a * imag_b, axis=0)
    return jnp.concatenate([real_sum, imag_sum], axis=-1)


def pick_rows(rows, block):
    picks = (rows[:, None] == lax.iota(jnp.int32, block.shape[1])[None, :]).astype(block.dtype)
    return jnp.einsum("gp,spk->sgk", picks, block, preferred_element_type=jnp.float32)


def on_device(samples, offsets, bad_mask):
    channels, segments, length = samples.shape
    half_len = length // 2
    stops = offsets.shape[0]
    spectrum = jnp.dot(
        jnp.swapaxes(samples, 0, 1).reshape(segments * channels, length),
        forward_table(length),
        preferred_element_type=jnp.float32,
    ).reshape(segments, channels, length)
    keep = (1 - bad_mask).astype(jnp.float32)
    white = whiten(spectrum, keep[None, :, None], half_len)
    first_rep = lax.axis_index("rep") == 0
    dc_imag = lax.broadcasted_iota(jnp.int32, white.shape, 2) == half_len
    moving = white.at[:stops, :, half_len].set(offsets.astype(jnp.bfloat16))
    back_table = inverse_table(length, LAGS)
    lags = []
    for stop in range(1, stops + 1):
        moving, lags = lax.optimization_barrier((along(moving, 1, -1), lags))
        arrived = jnp.where(dc_imag, jnp.zeros_like(moving), moving)
        rows = jnp.where(first_rep, offsets[stop - 1], moving[stop - 1, :, half_len].astype(jnp.int32))
        paired = jnp.where(first_rep, white, arrived).astype(jnp.float32)
        partner = pick_rows(rows, jnp.where(first_rep, arrived, white))
        lags.append(
            jnp.dot(
                cross_spectrum(paired, partner, half_len),
                back_table,
                precision=lax.Precision.HIGHEST,
                preferred_element_type=jnp.float32,
            )
        )
    mine = jnp.stack(lags, axis=1)
    across = jnp.stack([along(piece, -d, d, flip=True) for d, piece in enumerate(lags, 1)], axis=1)
    beside = jnp.stack([along(piece, -d, d) for d, piece in enumerate(lags, 1)], axis=1)
    other = swapped(mine, "rep")
    scale = 1.0 / math.sqrt(segments * lax.axis_size("rep") * half_len)
    correlations = jnp.where(first_rep, mine + across, other + beside) * scale
    mirrored = (jnp.where(first_rep, beside + other, across + mine) * scale)[:, :, ::-1]
    return (correlations, mirrored)

def solution(mesh):
    return jax.shard_map(
        on_device,
        mesh=mesh,
        in_specs=(P("blk", "rep", None), P(None, "blk"), P("blk")),
        out_specs=(P("blk", None, None), P("blk", None, None)),
        check_vma=False,
    )
```

```python
import math

import jax
import jax.numpy as jnp
from jax import lax
from jax.sharding import PartitionSpec as P

LAGS = 128


def shifted(x, axis, by):
    length = lax.axis_size(axis)
    return lax.ppermute(x, axis, [(i, (i + by) % length) for i in range(length)])


def swapped(x, axis):
    length = lax.axis_size(axis)
    return lax.ppermute(x, axis, [(i, i ^ 1) for i in range(length)])


def cos_sin(phase, length):
    angle = phase.astype(jnp.float32) * (2.0 * math.pi / length)
    return jnp.cos(angle), jnp.sin(angle)


def forward_table(length):
    half_len = length // 2
    lo_len = 64
    hi_len = length // lo_len
    bin_idx = lax.iota(jnp.int32, half_len)
    hi_idx = lax.iota(jnp.int32, hi_len) * lo_len
    lo_idx = lax.iota(jnp.int32, lo_len)
    cos_hi, sin_hi = cos_sin(hi_idx[:, None] * bin_idx[None, :] % length, length)
    cos_lo, sin_lo = cos_sin(lo_idx[:, None] * bin_idx[None, :] % length, length)
    cos_hi, sin_hi = cos_hi[:, None, :], sin_hi[:, None, :]
    cos_lo, sin_lo = cos_lo[None, :, :], sin_lo[None, :, :]
    cos_t = cos_hi * cos_lo - sin_hi * sin_lo
    sin_t = sin_hi * cos_lo + cos_hi * sin_lo
    table = jnp.concatenate([cos_t, -sin_t], axis=-1)
    return table.reshape(length, length).astype(jnp.bfloat16)


def inverse_table(length, lag_half):
    half_len = length // 2
    lo_len = 32
    hi_len = half_len // lo_len
    lag_idx = (lax.iota(jnp.int32, 2 * lag_half + 1) - lag_half) % length
    hi_idx = lax.iota(jnp.int32, hi_len) * lo_len
    lo_idx = lax.iota(jnp.int32, lo_len)
    cos_hi, sin_hi = cos_sin(hi_idx[:, None] * lag_idx[None, :] % length, length)
    cos_lo, sin_lo = cos_sin(lo_idx[:, None] * lag_idx[None, :] % length, length)
    cos_hi, sin_hi = cos_hi[:, None, :], sin_hi[:, None, :]
    cos_lo, sin_lo = cos_lo[None, :, :], sin_lo[None, :, :]
    cos_t = (cos_hi * cos_lo - sin_hi * sin_lo).reshape(half_len, -1)
    sin_t = (sin_hi * cos_lo + cos_hi * sin_lo).reshape(half_len, -1)
    return jnp.concatenate([cos_t, -sin_t], axis=0)


def whiten(spectrum, keep, half_len):
    power = jnp.sum(spectrum * spectrum, axis=-1, keepdims=True) / half_len
    return (spectrum * lax.rsqrt(power + 1e-06) * keep).astype(jnp.bfloat16)


def cross_spectrum(local, partner, half_len):
    real_a, imag_a = (local[..., :half_len], local[..., half_len:])
    real_b, imag_b = (partner[..., :half_len], partner[..., half_len:])
    real_sum = jnp.sum(real_a * real_b + imag_a * imag_b, axis=0)
    imag_sum = jnp.sum(imag_a * real_b - real_a * imag_b, axis=0)
    return jnp.concatenate([real_sum, imag_sum], axis=-1)


def pick_rows(rows, block):
    picks = (rows[:, None] == lax.iota(jnp.int32, block.shape[1])[None, :]).astype(block.dtype)
    return jnp.einsum("gp,spk->sgk", picks, block, preferred_element_type=jnp.float32)


def on_device(samples, offsets, bad_mask):
    channels, segments, length = samples.shape
    half_len = length // 2
    stops = offsets.shape[0]
    spectrum = jnp.dot(
        jnp.swapaxes(samples, 0, 1).reshape(segments * channels, length),
        forward_table(length),
        preferred_element_type=jnp.float32,
    ).reshape(segments, channels, length)
    keep = (1 - bad_mask).astype(jnp.float32)
    white = whiten(spectrum, keep[None, :, None], half_len)
    split = segments // 2
    ahead = white[:split]
    behind = white[split:]
    ahead_f32 = ahead.astype(jnp.float32)
    dc_imag = lax.broadcasted_iota(jnp.int32, behind.shape, 2) == half_len
    moving_ahead = ahead
    moving_behind = behind.at[:stops, :, half_len].set(offsets.astype(jnp.bfloat16))
    back_table = inverse_table(length, LAGS)

    def lags_of(stop, earlier, later):
        own = cross_spectrum(ahead_f32, pick_rows(offsets[stop - 1], earlier), half_len)
        later_offsets = later[stop - 1, :, half_len].astype(jnp.int32)
        later = jnp.where(dc_imag, jnp.zeros_like(later), later).astype(jnp.float32)
        later = cross_spectrum(later, pick_rows(later_offsets, behind), half_len)
        return jnp.dot(
            jnp.concatenate([own, later], axis=0),
            back_table,
            precision=lax.Precision.HIGHEST,
            preferred_element_type=jnp.float32,
        )

    near = stops // 2
    first = lax.optimization_barrier(
        tuple(shifted(moving_ahead, "blk", d) for d in range(1, near + 1))
        + tuple(shifted(moving_behind, "blk", -d) for d in range(1, near + 1))
    )
    lags = [lags_of(d, first[d - 1], first[near + d - 1]) for d in range(1, near + 1)]
    early = [(shifted(lags[0][channels:], "blk", 1), shifted(lags[0][:channels], "blk", -1))]

    def packed(bulk, piece):
        head = piece.astype(jnp.bfloat16)
        rest = (piece - head.astype(jnp.float32)).astype(jnp.bfloat16)
        flat = jnp.concatenate([head.reshape(-1), rest.reshape(-1)])
        flat = jnp.pad(flat, (0, channels * length - flat.shape[0]))
        return jnp.concatenate([bulk, flat.reshape(1, channels, length)], axis=0)

    def unpacked(bulk):
        flat = bulk[-1].reshape(-1)
        size = channels * back_table.shape[1]
        head = flat[:size].astype(jnp.float32) + flat[size:2 * size].astype(jnp.float32)
        return bulk[:-1], head.reshape(channels, -1)

    far_ahead, far_behind, early = lax.optimization_barrier(
        (
            shifted(packed(jnp.concatenate(first[:near], axis=0), lags[1][channels:]), "blk", near),
            shifted(packed(jnp.concatenate(first[near:], axis=0), lags[1][:channels]), "blk", -near),
            early,
        )
    )
    far_ahead, from_two_earlier = unpacked(far_ahead)
    far_behind, from_two_later = unpacked(far_behind)
    early = early + [(from_two_earlier, from_two_later)]
    for d in range(near + 1, stops + 1):
        at = (d - near - 1) * split
        lags.append(lags_of(d, far_ahead[at:at + split], far_behind[at:at + split]))
    late = [(shifted(lags[d - 1][channels:], "blk", d), shifted(lags[d - 1][:channels], "blk", -d)) for d in
            range(near + 1, stops + 1)]
    own_parts = [piece[:channels] for piece in lags]
    later_parts = [piece[channels:] for piece in lags]
    from_earlier = [pair[0] for pair in early + late]
    from_later = [pair[1] for pair in early + late]
    corr_part = jnp.stack(own_parts, axis=1) + jnp.stack(from_earlier, axis=1)
    mirror_part = jnp.stack(from_later, axis=1) + jnp.stack(later_parts, axis=1)
    parts = jnp.stack([corr_part, mirror_part], axis=0)
    summed = parts + swapped(parts, "rep")
    scale = 1.0 / math.sqrt(segments * lax.axis_size("rep") * half_len)
    correlations = summed[0] * scale
    mirrored = (summed[1] * scale)[:, :, ::-1]
    return (correlations, mirrored)


def solution(mesh):
    return jax.shard_map(
        on_device,
        mesh=mesh,
        in_specs=(P("blk", "rep", None), P(None, "blk"), P("blk")),
        out_specs=(P("blk", None, None), P("blk", None, None)),
        check_vma=False,
    )
```

```python
import math

import jax
import jax.numpy as jnp
from jax import lax
from jax.sharding import PartitionSpec as P

LAGS = 128


def shifted(x, axis, by):
    length = lax.axis_size(axis)
    return lax.ppermute(x, axis, [(i, (i + by) % length) for i in range(length)])


def swapped(x, axis):
    length = lax.axis_size(axis)
    return lax.ppermute(x, axis, [(i, i ^ 1) for i in range(length)])


def along(x, first_by, second_by, flip=False):
    blocks = lax.axis_size("blk")
    land = 1 if flip else 0
    perm = [(b * 2, ((b + first_by) % blocks) * 2 + land) for b in range(blocks)]
    perm += [(b * 2 + 1, ((b + second_by) % blocks) * 2 + 1 - land) for b in range(blocks)]
    return lax.ppermute(x, ("blk", "rep"), perm)


def cos_sin(phase, length):
    angle = phase.astype(jnp.float32) * (2.0 * math.pi / length)
    return jnp.cos(angle), jnp.sin(angle)


def forward_table(length):
    half_len = length // 2
    lo_len = 64
    hi_len = length // lo_len
    bin_idx = lax.iota(jnp.int32, half_len)
    hi_idx = lax.iota(jnp.int32, hi_len) * lo_len
    lo_idx = lax.iota(jnp.int32, lo_len)
    cos_hi, sin_hi = cos_sin(hi_idx[:, None] * bin_idx[None, :] % length, length)
    cos_lo, sin_lo = cos_sin(lo_idx[:, None] * bin_idx[None, :] % length, length)
    cos_hi, sin_hi = cos_hi[:, None, :], sin_hi[:, None, :]
    cos_lo, sin_lo = cos_lo[None, :, :], sin_lo[None, :, :]
    cos_t = cos_hi * cos_lo - sin_hi * sin_lo
    sin_t = sin_hi * cos_lo + cos_hi * sin_lo
    table = jnp.concatenate([cos_t, -sin_t], axis=-1)
    return table.reshape(length, length).astype(jnp.bfloat16)


def inverse_table(length, lag_half):
    half_len = length // 2
    lo_len = 32
    hi_len = half_len // lo_len
    lag_idx = (lax.iota(jnp.int32, 2 * lag_half + 1) - lag_half) % length
    hi_idx = lax.iota(jnp.int32, hi_len) * lo_len
    lo_idx = lax.iota(jnp.int32, lo_len)
    cos_hi, sin_hi = cos_sin(hi_idx[:, None] * lag_idx[None, :] % length, length)
    cos_lo, sin_lo = cos_sin(lo_idx[:, None] * lag_idx[None, :] % length, length)
    cos_hi, sin_hi = cos_hi[:, None, :], sin_hi[:, None, :]
    cos_lo, sin_lo = cos_lo[None, :, :], sin_lo[None, :, :]
    cos_t = (cos_hi * cos_lo - sin_hi * sin_lo).reshape(half_len, -1)
    sin_t = (sin_hi * cos_lo + cos_hi * sin_lo).reshape(half_len, -1)
    return jnp.concatenate([cos_t, -sin_t], axis=0)


def whiten(spectrum, keep, half_len):
    power = jnp.sum(spectrum * spectrum, axis=-1, keepdims=True) / half_len
    return (spectrum * lax.rsqrt(power + 1e-06) * keep).astype(jnp.bfloat16)


def cross_spectrum(local, partner, half_len):
    real_a, imag_a = (local[..., :half_len], local[..., half_len:])
    real_b, imag_b = (partner[..., :half_len], partner[..., half_len:])
    real_sum = jnp.sum(real_a * real_b + imag_a * imag_b, axis=0)
    imag_sum = jnp.sum(imag_a * real_b - real_a * imag_b, axis=0)
    return jnp.concatenate([real_sum, imag_sum], axis=-1)


def pick_rows(rows, block):
    picks = (rows[:, None] == lax.iota(jnp.int32, block.shape[1])[None, :]).astype(block.dtype)
    return jnp.einsum("gp,spk->sgk", picks, block, preferred_element_type=jnp.float32)


def on_device(samples, offsets, bad_mask):
    channels, segments, length = samples.shape
    half_len = length // 2
    stops = offsets.shape[0]
    spectrum = jnp.dot(
        jnp.swapaxes(samples, 0, 1).reshape(segments * channels, length),
        forward_table(length),
        preferred_element_type=jnp.float32,
    ).reshape(segments, channels, length)
    keep = (1 - bad_mask).astype(jnp.float32)
    white = whiten(spectrum, keep[None, :, None], half_len)
    first_rep = lax.axis_index("rep") == 0
    dc_imag = lax.broadcasted_iota(jnp.int32, white.shape, 2) == half_len
    moving = white.at[:stops, :, half_len].set(offsets.astype(jnp.bfloat16))
    back_table = inverse_table(length, LAGS)
    lags = []
    for stop in range(1, stops + 1):
        moving, lags = lax.optimization_barrier((along(moving, 1, -1), lags))
        arrived = jnp.where(dc_imag, jnp.zeros_like(moving), moving)
        rows = jnp.where(first_rep, offsets[stop - 1], moving[stop - 1, :, half_len].astype(jnp.int32))
        paired = jnp.where(first_rep, white, arrived).astype(jnp.float32)
        partner = pick_rows(rows, jnp.where(first_rep, arrived, white))
        lags.append(
            jnp.dot(
                cross_spectrum(paired, partner, half_len),
                back_table,
                precision=lax.Precision.HIGHEST,
                preferred_element_type=jnp.float32,
            )
        )
    mine = jnp.stack(lags, axis=1)
    across = jnp.stack([along(piece, -d, d, flip=True) for d, piece in enumerate(lags, 1)], axis=1)
    done_here = jnp.where(first_rep, mine + across, across + mine)
    other = swapped(done_here, "rep")
    scale = 1.0 / math.sqrt(segments * lax.axis_size("rep") * half_len)
    correlations = jnp.where(first_rep, done_here, other) * scale
    mirrored = (jnp.where(first_rep, other, done_here) * scale)[:, :, ::-1]
    return (correlations, mirrored)

def solution(mesh):
    return jax.shard_map(
        on_device,
        mesh=mesh,
        in_specs=(P("blk", "rep", None), P(None, "blk"), P("blk")),
        out_specs=(P("blk", None, None), P("blk", None, None)),
        check_vma=False,
    )
```

```python
import math

import jax
import jax.numpy as jnp
from jax import lax
from jax.sharding import PartitionSpec as P

LAGS = 128


def shifted(x, axis, by):
    length = lax.axis_size(axis)
    return lax.ppermute(x, axis, [(i, (i + by) % length) for i in range(length)])


def swapped(x, axis):
    length = lax.axis_size(axis)
    return lax.ppermute(x, axis, [(i, i ^ 1) for i in range(length)])


def cos_sin(phase, length):
    angle = phase.astype(jnp.float32) * (2.0 * math.pi / length)
    return jnp.cos(angle), jnp.sin(angle)


def forward_table(length):
    half_len = length // 2
    lo_len = 64
    hi_len = length // lo_len
    bin_idx = lax.iota(jnp.int32, half_len)
    hi_idx = lax.iota(jnp.int32, hi_len) * lo_len
    lo_idx = lax.iota(jnp.int32, lo_len)
    cos_hi, sin_hi = cos_sin(hi_idx[:, None] * bin_idx[None, :] % length, length)
    cos_lo, sin_lo = cos_sin(lo_idx[:, None] * bin_idx[None, :] % length, length)
    cos_hi, sin_hi = cos_hi[:, None, :], sin_hi[:, None, :]
    cos_lo, sin_lo = cos_lo[None, :, :], sin_lo[None, :, :]
    cos_t = cos_hi * cos_lo - sin_hi * sin_lo
    sin_t = sin_hi * cos_lo + cos_hi * sin_lo
    table = jnp.concatenate([cos_t, -sin_t], axis=-1)
    return table.reshape(length, length).astype(jnp.bfloat16)


def inverse_table(length, lag_half):
    half_len = length // 2
    lo_len = 32
    hi_len = half_len // lo_len
    lag_idx = (lax.iota(jnp.int32, 2 * lag_half + 1) - lag_half) % length
    hi_idx = lax.iota(jnp.int32, hi_len) * lo_len
    lo_idx = lax.iota(jnp.int32, lo_len)
    cos_hi, sin_hi = cos_sin(hi_idx[:, None] * lag_idx[None, :] % length, length)
    cos_lo, sin_lo = cos_sin(lo_idx[:, None] * lag_idx[None, :] % length, length)
    cos_hi, sin_hi = cos_hi[:, None, :], sin_hi[:, None, :]
    cos_lo, sin_lo = cos_lo[None, :, :], sin_lo[None, :, :]
    cos_t = (cos_hi * cos_lo - sin_hi * sin_lo).reshape(half_len, -1)
    sin_t = (sin_hi * cos_lo + cos_hi * sin_lo).reshape(half_len, -1)
    return jnp.concatenate([cos_t, -sin_t], axis=0)


def whiten(spectrum, keep, half_len):
    power = jnp.sum(spectrum * spectrum, axis=-1, keepdims=True) / half_len
    return (spectrum * lax.rsqrt(power + 1e-06) * keep).astype(jnp.bfloat16)


def cross_spectrum(local, partner, half_len):
    real_a, imag_a = (local[..., :half_len], local[..., half_len:])
    real_b, imag_b = (partner[..., :half_len], partner[..., half_len:])
    real_sum = jnp.sum(real_a * real_b + imag_a * imag_b, axis=0)
    imag_sum = jnp.sum(imag_a * real_b - real_a * imag_b, axis=0)
    return jnp.concatenate([real_sum, imag_sum], axis=-1)


def pick_rows(rows, block):
    picks = (rows[:, None] == lax.iota(jnp.int32, block.shape[1])[None, :]).astype(block.dtype)
    return jnp.einsum("gp,spk->sgk", picks, block, preferred_element_type=jnp.float32)


def on_device(samples, offsets, bad_mask):
    channels, segments, length = samples.shape
    half_len = length // 2
    stops = offsets.shape[0]
    spectrum = jnp.dot(
        jnp.swapaxes(samples, 0, 1).reshape(segments * channels, length),
        forward_table(length),
        preferred_element_type=jnp.float32,
    ).reshape(segments, channels, length)
    keep = (1 - bad_mask).astype(jnp.float32)
    white = whiten(spectrum, keep[None, :, None], half_len)
    split = segments // 2
    ahead = white[:split]
    behind = white[split:]
    ahead_f32 = ahead.astype(jnp.float32)
    dc_imag = lax.broadcasted_iota(jnp.int32, behind.shape, 2) == half_len
    moving_ahead = ahead
    moving_behind = behind.at[:stops, :, half_len].set(offsets.astype(jnp.bfloat16))
    back_table = inverse_table(length, LAGS)

    def lags_of(stop, earlier, later):
        own = cross_spectrum(ahead_f32, pick_rows(offsets[stop - 1], earlier), half_len)
        later_offsets = later[stop - 1, :, half_len].astype(jnp.int32)
        later = jnp.where(dc_imag, jnp.zeros_like(later), later).astype(jnp.float32)
        later = cross_spectrum(later, pick_rows(later_offsets, behind), half_len)
        return jnp.concatenate([own, later], axis=0)

    def lags_of_stops(crosses):
        rows = crosses[0].shape[0]
        lags = jnp.dot(
            jnp.concatenate(crosses, axis=0),
            back_table,
            precision=lax.Precision.HIGH,
            preferred_element_type=jnp.float32,
        )
        return [lags[i * rows:(i + 1) * rows] for i in range(len(crosses))]

    near = stops // 2
    first = lax.optimization_barrier(
        tuple(shifted(moving_ahead, "blk", d) for d in range(1, near + 1))
        + tuple(shifted(moving_behind, "blk", -d) for d in range(1, near + 1))
    )
    lags = lags_of_stops([lags_of(d, first[d - 1], first[near + d - 1]) for d in range(1, near + 1)])
    early = [
        (shifted(piece[channels:], "blk", d), shifted(piece[:channels], "blk", -d)) for d, piece in enumerate(lags, 1)
    ]
    far_ahead, far_behind, early = lax.optimization_barrier(
        (
            shifted(jnp.concatenate(first[:near], axis=0), "blk", near),
            shifted(jnp.concatenate(first[near:], axis=0), "blk", -near),
            early,
        )
    )
    lags += lags_of_stops(
        [
            lags_of(d, far_ahead[(d - near - 1) * split:(d - near) * split], far_behind[(d - near - 1) * split:(d - near) * split])
            for d in range(near + 1, stops + 1)
        ]
    )
    late = [(shifted(lags[d - 1][channels:], "blk", d), shifted(lags[d - 1][:channels], "blk", -d)) for d in
            range(near + 1, stops + 1)]
    own_parts = [piece[:channels] for piece in lags]
    later_parts = [piece[channels:] for piece in lags]
    from_earlier = [pair[0] for pair in early + late]
    from_later = [pair[1] for pair in early + late]
    corr_part = jnp.stack(own_parts, axis=1) + jnp.stack(from_earlier, axis=1)
    mirror_part = jnp.stack(from_later, axis=1) + jnp.stack(later_parts, axis=1)
    parts = jnp.stack([corr_part, mirror_part], axis=0)
    summed = parts + swapped(parts, "rep")
    scale = 1.0 / math.sqrt(segments * lax.axis_size("rep") * half_len)
    correlations = summed[0] * scale
    mirrored = (summed[1] * scale)[:, :, ::-1]
    return (correlations, mirrored)


def solution(mesh):
    return jax.shard_map(
        on_device,
        mesh=mesh,
        in_specs=(P("blk", "rep", None), P(None, "blk"), P("blk")),
        out_specs=(P("blk", None, None), P("blk", None, None)),
        check_vma=False,
    )
```

```python
import math

import jax
import jax.numpy as jnp
from jax import lax
from jax.sharding import PartitionSpec as P

LAGS = 128


def shifted(x, axis, by):
    length = lax.axis_size(axis)
    return lax.ppermute(x, axis, [(i, (i + by) % length) for i in range(length)])


def swapped(x, axis):
    length = lax.axis_size(axis)
    return lax.ppermute(x, axis, [(i, i ^ 1) for i in range(length)])


def cos_sin(phase, length):
    angle = phase.astype(jnp.float32) * (2.0 * math.pi / length)
    return jnp.cos(angle), jnp.sin(angle)


def forward_table(length):
    half_len = length // 2
    lo_len = 64
    hi_len = length // lo_len
    bin_idx = lax.iota(jnp.int32, half_len)
    hi_idx = lax.iota(jnp.int32, hi_len) * lo_len
    lo_idx = lax.iota(jnp.int32, lo_len)
    cos_hi, sin_hi = cos_sin(hi_idx[:, None] * bin_idx[None, :] % length, length)
    cos_lo, sin_lo = cos_sin(lo_idx[:, None] * bin_idx[None, :] % length, length)
    cos_hi, sin_hi = cos_hi[:, None, :], sin_hi[:, None, :]
    cos_lo, sin_lo = cos_lo[None, :, :], sin_lo[None, :, :]
    cos_t = cos_hi * cos_lo - sin_hi * sin_lo
    sin_t = sin_hi * cos_lo + cos_hi * sin_lo
    table = jnp.concatenate([cos_t, -sin_t], axis=-1)
    return table.reshape(length, length).astype(jnp.bfloat16)


def inverse_table(length, lag_half):
    half_len = length // 2
    lo_len = 32
    hi_len = half_len // lo_len
    lag_idx = (lax.iota(jnp.int32, 2 * lag_half + 1) - lag_half) % length
    hi_idx = lax.iota(jnp.int32, hi_len) * lo_len
    lo_idx = lax.iota(jnp.int32, lo_len)
    cos_hi, sin_hi = cos_sin(hi_idx[:, None] * lag_idx[None, :] % length, length)
    cos_lo, sin_lo = cos_sin(lo_idx[:, None] * lag_idx[None, :] % length, length)
    cos_hi, sin_hi = cos_hi[:, None, :], sin_hi[:, None, :]
    cos_lo, sin_lo = cos_lo[None, :, :], sin_lo[None, :, :]
    cos_t = (cos_hi * cos_lo - sin_hi * sin_lo).reshape(half_len, -1)
    sin_t = (sin_hi * cos_lo + cos_hi * sin_lo).reshape(half_len, -1)
    return jnp.concatenate([cos_t, -sin_t], axis=0)


def whiten(spectrum, keep, half_len):
    power = jnp.sum(spectrum * spectrum, axis=-1, keepdims=True) / half_len
    return (spectrum * lax.rsqrt(power + 1e-06) * keep).astype(jnp.bfloat16)


def cross_spectrum(local, partner, half_len):
    real_a, imag_a = (local[..., :half_len], local[..., half_len:])
    real_b, imag_b = (partner[..., :half_len], partner[..., half_len:])
    real_sum = jnp.sum(real_a * real_b + imag_a * imag_b, axis=0)
    imag_sum = jnp.sum(imag_a * real_b - real_a * imag_b, axis=0)
    return jnp.concatenate([real_sum, imag_sum], axis=-1)


def pick_rows(rows, block):
    picks = (rows[:, None] == lax.iota(jnp.int32, block.shape[1])[None, :]).astype(block.dtype)
    return jnp.einsum("gp,spk->sgk", picks, block, preferred_element_type=jnp.float32)


def on_device(samples, offsets, bad_mask):
    channels, segments, length = samples.shape
    half_len = length // 2
    stops = offsets.shape[0]
    spectrum = jnp.dot(
        jnp.swapaxes(samples, 0, 1).reshape(segments * channels, length),
        forward_table(length),
        preferred_element_type=jnp.float32,
    ).reshape(segments, channels, length)
    keep = (1 - bad_mask).astype(jnp.float32)
    white = whiten(spectrum, keep[None, :, None], half_len)
    split = segments // 2
    ahead = white[:split]
    behind = white[split:]
    ahead_f32 = ahead.astype(jnp.float32)
    dc_imag = lax.broadcasted_iota(jnp.int32, behind.shape, 2) == half_len
    moving_ahead = ahead
    moving_behind = behind.at[:stops, :, half_len].set(offsets.astype(jnp.bfloat16))
    back_table = inverse_table(length, LAGS)

    def lags_of(stop, earlier, later):
        own = cross_spectrum(ahead_f32, pick_rows(offsets[stop - 1], earlier), half_len)
        later_offsets = later[stop - 1, :, half_len].astype(jnp.int32)
        later = jnp.where(dc_imag, jnp.zeros_like(later), later).astype(jnp.float32)
        later = cross_spectrum(later, pick_rows(later_offsets, behind), half_len)
        return jnp.dot(
            jnp.concatenate([own, later], axis=0),
            back_table,
            precision=lax.Precision.HIGH,
            preferred_element_type=jnp.float32,
        )

    near = stops // 2
    first = lax.optimization_barrier(
        tuple(shifted(moving_ahead, "blk", d) for d in range(1, near + 1))
        + tuple(shifted(moving_behind, "blk", -d) for d in range(1, near + 1))
    )
    lags = [lags_of(d, first[d - 1], first[near + d - 1]) for d in range(1, near + 1)]
    early = [
        (shifted(piece[channels:], "blk", d), shifted(piece[:channels], "blk", -d)) for d, piece in enumerate(lags, 1)
    ]
    far_ahead, far_behind, early = lax.optimization_barrier(
        (
            shifted(jnp.concatenate(first[:near], axis=0), "blk", near),
            shifted(jnp.concatenate(first[near:], axis=0), "blk", -near),
            early,
        )
    )
    for d in range(near + 1, stops + 1):
        at = (d - near - 1) * split
        lags.append(lags_of(d, far_ahead[at:at + split], far_behind[at:at + split]))
    late = [(shifted(lags[d - 1][channels:], "blk", d), shifted(lags[d - 1][:channels], "blk", -d)) for d in
            range(near + 1, stops + 1)]
    own_parts = [piece[:channels] for piece in lags]
    later_parts = [piece[channels:] for piece in lags]
    from_earlier = [pair[0] for pair in early + late]
    from_later = [pair[1] for pair in early + late]
    corr_part = jnp.stack(own_parts, axis=1) + jnp.stack(from_earlier, axis=1)
    mirror_part = jnp.stack(from_later, axis=1) + jnp.stack(later_parts, axis=1)
    parts = jnp.stack([corr_part, mirror_part], axis=0)
    summed = parts + swapped(parts, "rep")
    scale = 1.0 / math.sqrt(segments * lax.axis_size("rep") * half_len)
    correlations = summed[0] * scale
    mirrored = (summed[1] * scale)[:, :, ::-1]
    return (correlations, mirrored)


def solution(mesh):
    return jax.shard_map(
        on_device,
        mesh=mesh,
        in_specs=(P("blk", "rep", None), P(None, "blk"), P("blk")),
        out_specs=(P("blk", None, None), P("blk", None, None)),
        check_vma=False,
    )
```

```python
import math

import jax
import jax.numpy as jnp
from jax import lax
from jax.sharding import PartitionSpec as P

LAGS = 128


def shifted(x, axis, by):
    length = lax.axis_size(axis)
    return lax.ppermute(x, axis, [(i, (i + by) % length) for i in range(length)])


def swapped(x, axis):
    length = lax.axis_size(axis)
    return lax.ppermute(x, axis, [(i, i ^ 1) for i in range(length)])


def cos_sin(phase, length):
    angle = phase.astype(jnp.float32) * (2.0 * math.pi / length)
    return jnp.cos(angle), jnp.sin(angle)


def forward_table(length):
    half_len = length // 2
    lo_len = 64
    hi_len = length // lo_len
    bin_idx = lax.iota(jnp.int32, half_len)
    hi_idx = lax.iota(jnp.int32, hi_len) * lo_len
    lo_idx = lax.iota(jnp.int32, lo_len)
    cos_hi, sin_hi = cos_sin(hi_idx[:, None] * bin_idx[None, :] % length, length)
    cos_lo, sin_lo = cos_sin(lo_idx[:, None] * bin_idx[None, :] % length, length)
    cos_hi, sin_hi = cos_hi[:, None, :], sin_hi[:, None, :]
    cos_lo, sin_lo = cos_lo[None, :, :], sin_lo[None, :, :]
    cos_t = cos_hi * cos_lo - sin_hi * sin_lo
    sin_t = sin_hi * cos_lo + cos_hi * sin_lo
    table = jnp.concatenate([cos_t, -sin_t], axis=-1)
    return table.reshape(length, length).astype(jnp.bfloat16)


def inverse_table(length, lag_half):
    half_len = length // 2
    lo_len = 32
    hi_len = half_len // lo_len
    lag_idx = (lax.iota(jnp.int32, 2 * lag_half + 1) - lag_half) % length
    hi_idx = lax.iota(jnp.int32, hi_len) * lo_len
    lo_idx = lax.iota(jnp.int32, lo_len)
    cos_hi, sin_hi = cos_sin(hi_idx[:, None] * lag_idx[None, :] % length, length)
    cos_lo, sin_lo = cos_sin(lo_idx[:, None] * lag_idx[None, :] % length, length)
    cos_hi, sin_hi = cos_hi[:, None, :], sin_hi[:, None, :]
    cos_lo, sin_lo = cos_lo[None, :, :], sin_lo[None, :, :]
    cos_t = (cos_hi * cos_lo - sin_hi * sin_lo).reshape(half_len, -1)
    sin_t = (sin_hi * cos_lo + cos_hi * sin_lo).reshape(half_len, -1)
    return jnp.concatenate([cos_t, -sin_t], axis=0)


def whiten(spectrum, keep, half_len):
    power = jnp.sum(spectrum * spectrum, axis=-1, keepdims=True) / half_len
    return (spectrum * lax.rsqrt(power + 1e-06) * keep).astype(jnp.bfloat16)


def cross_spectrum(local, partner, half_len):
    real_a, imag_a = (local[..., :half_len], local[..., half_len:])
    real_b, imag_b = (partner[..., :half_len], partner[..., half_len:])
    real_sum = jnp.sum(real_a * real_b + imag_a * imag_b, axis=0)
    imag_sum = jnp.sum(imag_a * real_b - real_a * imag_b, axis=0)
    return jnp.concatenate([real_sum, imag_sum], axis=-1)


def pick_rows(rows, block):
    picks = (rows[:, None] == lax.iota(jnp.int32, block.shape[1])[None, :]).astype(block.dtype)
    return jnp.einsum("gp,spk->sgk", picks, block, preferred_element_type=jnp.float32)


def on_device(samples, offsets, bad_mask):
    channels, segments, length = samples.shape
    half_len = length // 2
    stops = offsets.shape[0]
    spectrum = jnp.dot(
        jnp.swapaxes(samples, 0, 1).reshape(segments * channels, length),
        forward_table(length),
        preferred_element_type=jnp.float32,
    ).reshape(segments, channels, length)
    keep = (1 - bad_mask).astype(jnp.float32)
    white = whiten(spectrum, keep[None, :, None], half_len)
    split = segments // 2
    ahead = white[:split]
    behind = white[split:]
    ahead_f32 = ahead.astype(jnp.float32)
    dc_imag = lax.broadcasted_iota(jnp.int32, behind.shape, 2) == half_len
    moving_ahead = ahead
    moving_behind = behind.at[:stops, :, half_len].set(offsets.astype(jnp.bfloat16))
    back_table = inverse_table(length, LAGS)

    def lags_of(stop, earlier, later):
        own = cross_spectrum(ahead_f32, pick_rows(offsets[stop - 1], earlier), half_len)
        later_offsets = later[stop - 1, :, half_len].astype(jnp.int32)
        later = jnp.where(dc_imag, jnp.zeros_like(later), later).astype(jnp.float32)
        later = cross_spectrum(later, pick_rows(later_offsets, behind), half_len)
        return jnp.concatenate([own, later], axis=0)

    def lags_of_stops(crosses):
        rows = crosses[0].shape[0]
        lags = jnp.dot(
            jnp.concatenate(crosses, axis=0),
            back_table,
            precision=lax.Precision.HIGH,
            preferred_element_type=jnp.float32,
        )
        return [lags[i * rows:(i + 1) * rows] for i in range(len(crosses))]

    near = stops // 2
    first = lax.optimization_barrier(
        tuple(shifted(moving_ahead, "blk", d) for d in range(1, near + 1))
        + tuple(shifted(moving_behind, "blk", -d) for d in range(1, near + 1))
    )
    lags = [lags_of_stops([lags_of(d, first[d - 1], first[near + d - 1])])[0] for d in range(1, near + 1)]
    early = [
        (shifted(piece[channels:], "blk", d), shifted(piece[:channels], "blk", -d)) for d, piece in enumerate(lags, 1)
    ]
    far_ahead, far_behind, early = lax.optimization_barrier(
        (
            shifted(jnp.concatenate(first[:near], axis=0), "blk", near),
            shifted(jnp.concatenate(first[near:], axis=0), "blk", -near),
            early,
        )
    )
    lags += lags_of_stops(
        [
            lags_of(d, far_ahead[(d - near - 1) * split:(d - near) * split], far_behind[(d - near - 1) * split:(d - near) * split])
            for d in range(near + 1, stops + 1)
        ]
    )
    late = [(shifted(lags[d - 1][channels:], "blk", d), shifted(lags[d - 1][:channels], "blk", -d)) for d in
            range(near + 1, stops + 1)]
    own_parts = [piece[:channels] for piece in lags]
    later_parts = [piece[channels:] for piece in lags]
    from_earlier = [pair[0] for pair in early + late]
    from_later = [pair[1] for pair in early + late]
    corr_part = jnp.stack(own_parts, axis=1) + jnp.stack(from_earlier, axis=1)
    mirror_part = jnp.stack(from_later, axis=1) + jnp.stack(later_parts, axis=1)
    parts = jnp.stack([corr_part, mirror_part], axis=0)
    summed = parts + swapped(parts, "rep")
    scale = 1.0 / math.sqrt(segments * lax.axis_size("rep") * half_len)
    correlations = summed[0] * scale
    mirrored = (summed[1] * scale)[:, :, ::-1]
    return (correlations, mirrored)


def solution(mesh):
    return jax.shard_map(
        on_device,
        mesh=mesh,
        in_specs=(P("blk", "rep", None), P(None, "blk"), P("blk")),
        out_specs=(P("blk", None, None), P("blk", None, None)),
        check_vma=False,
    )
```

```python
import math

import jax
import jax.numpy as jnp
from jax import lax
from jax.sharding import PartitionSpec as P

LAGS = 128


def shifted(x, axis, by):
    length = lax.axis_size(axis)
    return lax.ppermute(x, axis, [(i, (i + by) % length) for i in range(length)])


def swapped(x, axis):
    length = lax.axis_size(axis)
    return lax.ppermute(x, axis, [(i, i ^ 1) for i in range(length)])


def cos_sin(phase, length):
    angle = phase.astype(jnp.float32) * (2.0 * math.pi / length)
    return jnp.cos(angle), jnp.sin(angle)


def forward_table(length):
    half_len = length // 2
    lo_len = 64
    hi_len = length // lo_len
    bin_idx = lax.iota(jnp.int32, half_len)
    hi_idx = lax.iota(jnp.int32, hi_len) * lo_len
    lo_idx = lax.iota(jnp.int32, lo_len)
    cos_hi, sin_hi = cos_sin(hi_idx[:, None] * bin_idx[None, :] % length, length)
    cos_lo, sin_lo = cos_sin(lo_idx[:, None] * bin_idx[None, :] % length, length)
    cos_hi, sin_hi = cos_hi[:, None, :], sin_hi[:, None, :]
    cos_lo, sin_lo = cos_lo[None, :, :], sin_lo[None, :, :]
    cos_t = cos_hi * cos_lo - sin_hi * sin_lo
    sin_t = sin_hi * cos_lo + cos_hi * sin_lo
    table = jnp.concatenate([cos_t, -sin_t], axis=-1)
    return table.reshape(length, length).astype(jnp.bfloat16)


def inverse_table(length, lag_half):
    half_len = length // 2
    lo_len = 32
    hi_len = half_len // lo_len
    lag_idx = (lax.iota(jnp.int32, 2 * lag_half + 1) - lag_half) % length
    hi_idx = lax.iota(jnp.int32, hi_len) * lo_len
    lo_idx = lax.iota(jnp.int32, lo_len)
    cos_hi, sin_hi = cos_sin(hi_idx[:, None] * lag_idx[None, :] % length, length)
    cos_lo, sin_lo = cos_sin(lo_idx[:, None] * lag_idx[None, :] % length, length)
    cos_hi, sin_hi = cos_hi[:, None, :], sin_hi[:, None, :]
    cos_lo, sin_lo = cos_lo[None, :, :], sin_lo[None, :, :]
    cos_t = (cos_hi * cos_lo - sin_hi * sin_lo).reshape(half_len, -1)
    sin_t = (sin_hi * cos_lo + cos_hi * sin_lo).reshape(half_len, -1)
    return jnp.concatenate([cos_t, -sin_t], axis=0)


def whiten(spectrum, keep, half_len):
    power = jnp.sum(spectrum * spectrum, axis=-1, keepdims=True) / half_len
    return (spectrum * lax.rsqrt(power + 1e-06) * keep).astype(jnp.bfloat16)


def cross_spectrum(local, partner, half_len):
    real_a, imag_a = (local[..., :half_len], local[..., half_len:])
    real_b, imag_b = (partner[..., :half_len], partner[..., half_len:])
    real_sum = jnp.sum(real_a * real_b + imag_a * imag_b, axis=0)
    imag_sum = jnp.sum(imag_a * real_b - real_a * imag_b, axis=0)
    return jnp.concatenate([real_sum, imag_sum], axis=-1)


def pick_rows(rows, block):
    picks = (rows[:, None] == lax.iota(jnp.int32, block.shape[1])[None, :]).astype(block.dtype)
    return jnp.einsum("gp,spk->sgk", picks, block, preferred_element_type=jnp.float32)


def on_device(samples, offsets, bad_mask):
    channels, segments, length = samples.shape
    half_len = length // 2
    stops = offsets.shape[0]
    spectrum = jnp.einsum("csn,nk->sck", samples, forward_table(length), preferred_element_type=jnp.float32)
    keep = (1 - bad_mask).astype(jnp.float32)
    white = whiten(spectrum, keep[None, :, None], half_len)
    split = segments // 2
    ahead = white[:split]
    behind = white[split:]
    ahead_f32 = ahead.astype(jnp.float32)
    dc_imag = lax.broadcasted_iota(jnp.int32, behind.shape, 2) == half_len
    moving_ahead = ahead
    moving_behind = behind.at[:stops, :, half_len].set(offsets.astype(jnp.bfloat16))
    back_table = inverse_table(length, LAGS)

    def lags_of(stop, earlier, later):
        own = cross_spectrum(ahead_f32, pick_rows(offsets[stop - 1], earlier), half_len)
        later_offsets = later[stop - 1, :, half_len].astype(jnp.int32)
        later = jnp.where(dc_imag, jnp.zeros_like(later), later).astype(jnp.float32)
        later = cross_spectrum(later, pick_rows(later_offsets, behind), half_len)
        return jnp.concatenate([own, later], axis=0)

    def lags_of_stops(crosses):
        rows = crosses[0].shape[0]
        lags = jnp.dot(
            jnp.concatenate(crosses, axis=0),
            back_table,
            precision=lax.Precision.HIGH,
            preferred_element_type=jnp.float32,
        )
        return [lags[i * rows:(i + 1) * rows] for i in range(len(crosses))]

    near = stops // 2
    first = lax.optimization_barrier(
        tuple(shifted(moving_ahead, "blk", d) for d in range(1, near + 1))
        + tuple(shifted(moving_behind, "blk", -d) for d in range(1, near + 1))
    )
    lags = [lags_of_stops([lags_of(d, first[d - 1], first[near + d - 1])])[0] for d in range(1, near + 1)]
    early = [
        (shifted(piece[channels:], "blk", d), shifted(piece[:channels], "blk", -d)) for d, piece in enumerate(lags, 1)
    ]
    far_ahead, far_behind, early = lax.optimization_barrier(
        (
            shifted(jnp.concatenate(first[:near], axis=0), "blk", near),
            shifted(jnp.concatenate(first[near:], axis=0), "blk", -near),
            early,
        )
    )
    lags += lags_of_stops(
        [
            lags_of(d, far_ahead[(d - near - 1) * split:(d - near) * split], far_behind[(d - near - 1) * split:(d - near) * split])
            for d in range(near + 1, stops + 1)
        ]
    )
    late = [(shifted(lags[d - 1][channels:], "blk", d), shifted(lags[d - 1][:channels], "blk", -d)) for d in
            range(near + 1, stops + 1)]
    own_parts = [piece[:channels] for piece in lags]
    later_parts = [piece[channels:] for piece in lags]
    from_earlier = [pair[0] for pair in early + late]
    from_later = [pair[1] for pair in early + late]
    corr_part = jnp.stack(own_parts, axis=1) + jnp.stack(from_earlier, axis=1)
    mirror_part = jnp.stack(from_later, axis=1) + jnp.stack(later_parts, axis=1)
    parts = jnp.stack([corr_part, mirror_part], axis=0)
    summed = parts + swapped(parts, "rep")
    scale = 1.0 / math.sqrt(segments * lax.axis_size("rep") * half_len)
    correlations = summed[0] * scale
    mirrored = (summed[1] * scale)[:, :, ::-1]
    return (correlations, mirrored)


def solution(mesh):
    return jax.shard_map(
        on_device,
        mesh=mesh,
        in_specs=(P("blk", "rep", None), P(None, "blk"), P("blk")),
        out_specs=(P("blk", None, None), P("blk", None, None)),
        check_vma=False,
    )
```

```python
import math

import jax
import jax.numpy as jnp
from jax import lax
from jax.sharding import PartitionSpec as P

LAGS = 128


def shifted(x, axis, by):
    length = lax.axis_size(axis)
    return lax.ppermute(x, axis, [(i, (i + by) % length) for i in range(length)])


def swapped(x, axis):
    length = lax.axis_size(axis)
    return lax.ppermute(x, axis, [(i, i ^ 1) for i in range(length)])


def cos_sin(phase, length):
    angle = phase.astype(jnp.float32) * (2.0 * math.pi / length)
    return jnp.cos(angle), jnp.sin(angle)


def forward_table(length):
    half_len = length // 2
    lo_len = 64
    hi_len = length // lo_len
    bin_idx = lax.iota(jnp.int32, half_len)
    hi_idx = lax.iota(jnp.int32, hi_len) * lo_len
    lo_idx = lax.iota(jnp.int32, lo_len)
    cos_hi, sin_hi = cos_sin(hi_idx[:, None] * bin_idx[None, :] % length, length)
    cos_lo, sin_lo = cos_sin(lo_idx[:, None] * bin_idx[None, :] % length, length)
    cos_hi, sin_hi = cos_hi[:, None, :], sin_hi[:, None, :]
    cos_lo, sin_lo = cos_lo[None, :, :], sin_lo[None, :, :]
    cos_t = cos_hi * cos_lo - sin_hi * sin_lo
    sin_t = sin_hi * cos_lo + cos_hi * sin_lo
    table = jnp.concatenate([cos_t, -sin_t], axis=-1)
    return table.reshape(length, length).astype(jnp.bfloat16)


def inverse_table(length, lag_half):
    half_len = length // 2
    lo_len = 32
    hi_len = half_len // lo_len
    lag_idx = (lax.iota(jnp.int32, 2 * lag_half + 1) - lag_half) % length
    hi_idx = lax.iota(jnp.int32, hi_len) * lo_len
    lo_idx = lax.iota(jnp.int32, lo_len)
    cos_hi, sin_hi = cos_sin(hi_idx[:, None] * lag_idx[None, :] % length, length)
    cos_lo, sin_lo = cos_sin(lo_idx[:, None] * lag_idx[None, :] % length, length)
    cos_hi, sin_hi = cos_hi[:, None, :], sin_hi[:, None, :]
    cos_lo, sin_lo = cos_lo[None, :, :], sin_lo[None, :, :]
    cos_t = (cos_hi * cos_lo - sin_hi * sin_lo).reshape(half_len, -1)
    sin_t = (sin_hi * cos_lo + cos_hi * sin_lo).reshape(half_len, -1)
    return jnp.concatenate([cos_t, -sin_t], axis=0)


def whiten(spectrum, keep, half_len):
    power = jnp.sum(spectrum * spectrum, axis=-1, keepdims=True) / half_len
    return (spectrum * lax.rsqrt(power + 1e-06) * keep).astype(jnp.bfloat16)


def cross_spectrum(local, partner, half_len):
    real_a, imag_a = (local[..., :half_len], local[..., half_len:])
    real_b, imag_b = (partner[..., :half_len], partner[..., half_len:])
    real_sum = jnp.sum(real_a * real_b + imag_a * imag_b, axis=0)
    imag_sum = jnp.sum(imag_a * real_b - real_a * imag_b, axis=0)
    return jnp.concatenate([real_sum, imag_sum], axis=-1)


def pick_rows(rows, block):
    picks = (rows[:, None] == lax.iota(jnp.int32, block.shape[1])[None, :]).astype(block.dtype)
    return jnp.einsum("gp,spk->sgk", picks, block, preferred_element_type=jnp.float32)


def on_device(samples, offsets, bad_mask):
    channels, segments, length = samples.shape
    half_len = length // 2
    stops = offsets.shape[0]
    spectrum = jnp.dot(
        jnp.swapaxes(samples, 0, 1).reshape(segments * channels, length),
        forward_table(length),
        preferred_element_type=jnp.float32,
    ).reshape(segments, channels, length)
    keep = (1 - bad_mask).astype(jnp.float32)
    white = whiten(spectrum, keep[None, :, None], half_len)
    split = segments // 2
    ahead = white[:split]
    behind = white[split:]
    ahead_f32 = ahead.astype(jnp.float32)
    dc_imag = lax.broadcasted_iota(jnp.int32, behind.shape, 2) == half_len
    moving_ahead = ahead
    moving_behind = behind.at[:stops, :, half_len].set(offsets.astype(jnp.bfloat16))
    back_table = inverse_table(length, LAGS)

    def lags_of(stop, earlier, later):
        own = cross_spectrum(ahead_f32, pick_rows(offsets[stop - 1], earlier), half_len)
        later_offsets = later[stop - 1, :, half_len].astype(jnp.int32)
        later = jnp.where(dc_imag, jnp.zeros_like(later), later).astype(jnp.float32)
        later = cross_spectrum(later, pick_rows(later_offsets, behind), half_len)
        return jnp.concatenate([own, later], axis=0)

    def lags_of_stops(crosses):
        rows = crosses[0].shape[0]
        lags = jnp.dot(
            jnp.concatenate(crosses, axis=0),
            back_table,
            precision=lax.Precision.HIGH,
            preferred_element_type=jnp.float32,
        )
        return [lags[i * rows:(i + 1) * rows] for i in range(len(crosses))]

    near = stops // 2
    first = lax.optimization_barrier(
        tuple(shifted(moving_ahead, "blk", d) for d in range(1, near + 1))
        + tuple(shifted(moving_behind, "blk", -d) for d in range(1, near + 1))
    )
    lags = [lags_of_stops([lags_of(d, first[d - 1], first[near + d - 1])])[0] for d in range(1, near + 1)]
    early = [
        (shifted(piece[channels:], "blk", d), shifted(piece[:channels], "blk", -d)) for d, piece in enumerate(lags, 1)
    ]
    far_ahead, far_behind, early = lax.optimization_barrier(
        (
            shifted(jnp.concatenate(first[:near], axis=0), "blk", near),
            shifted(jnp.concatenate(first[near:], axis=0), "blk", -near),
            early,
        )
    )
    lags += lags_of_stops(
        [
            lags_of(d, far_ahead[(d - near - 1) * split:(d - near) * split], far_behind[(d - near - 1) * split:(d - near) * split])
            for d in range(near + 1, stops + 1)
        ]
    )
    late = [(shifted(lags[d - 1][channels:], "blk", d), shifted(lags[d - 1][:channels], "blk", -d)) for d in
            range(near + 1, stops + 1)]
    own_parts = [piece[:channels] for piece in lags]
    later_parts = [piece[channels:] for piece in lags]
    from_earlier = [pair[0] for pair in early + late]
    from_later = [pair[1] for pair in early + late]
    scale = 1.0 / math.sqrt(segments * lax.axis_size("rep") * half_len)
    corr_part = (jnp.stack(own_parts, axis=1) + jnp.stack(from_earlier, axis=1)) * scale
    mirror_part = ((jnp.stack(from_later, axis=1) + jnp.stack(later_parts, axis=1)) * scale)[:, :, ::-1]
    parts = jnp.stack([corr_part, mirror_part], axis=0)
    other = swapped(parts, "rep")
    return (parts[0] + other[0], parts[1] + other[1])


def solution(mesh):
    return jax.shard_map(
        on_device,
        mesh=mesh,
        in_specs=(P("blk", "rep", None), P(None, "blk"), P("blk")),
        out_specs=(P("blk", None, None), P("blk", None, None)),
        check_vma=False,
    )
```

```python
import math

import jax
import jax.numpy as jnp
from jax import lax
from jax.sharding import PartitionSpec as P

LAGS = 128


def shifted(x, axis, by):
    length = lax.axis_size(axis)
    return lax.ppermute(x, axis, [(i, (i + by) % length) for i in range(length)])


def swapped(x, axis):
    length = lax.axis_size(axis)
    return lax.ppermute(x, axis, [(i, i ^ 1) for i in range(length)])


def cos_sin(phase, length):
    angle = phase.astype(jnp.float32) * (2.0 * math.pi / length)
    return jnp.cos(angle), jnp.sin(angle)


def forward_table(length):
    half_len = length // 2
    lo_len = 64
    hi_len = length // lo_len
    bin_idx = lax.iota(jnp.int32, half_len)
    hi_idx = lax.iota(jnp.int32, hi_len) * lo_len
    lo_idx = lax.iota(jnp.int32, lo_len)
    cos_hi, sin_hi = cos_sin(hi_idx[:, None] * bin_idx[None, :] % length, length)
    cos_lo, sin_lo = cos_sin(lo_idx[:, None] * bin_idx[None, :] % length, length)
    cos_hi, sin_hi = cos_hi[:, None, :], sin_hi[:, None, :]
    cos_lo, sin_lo = cos_lo[None, :, :], sin_lo[None, :, :]
    cos_t = cos_hi * cos_lo - sin_hi * sin_lo
    sin_t = sin_hi * cos_lo + cos_hi * sin_lo
    table = jnp.concatenate([cos_t, -sin_t], axis=-1)
    return table.reshape(length, length).astype(jnp.bfloat16)


def inverse_table(length, lag_half):
    half_len = length // 2
    lo_len = 32
    hi_len = half_len // lo_len
    lag_idx = (lax.iota(jnp.int32, 2 * lag_half + 1) - lag_half) % length
    hi_idx = lax.iota(jnp.int32, hi_len) * lo_len
    lo_idx = lax.iota(jnp.int32, lo_len)
    cos_hi, sin_hi = cos_sin(hi_idx[:, None] * lag_idx[None, :] % length, length)
    cos_lo, sin_lo = cos_sin(lo_idx[:, None] * lag_idx[None, :] % length, length)
    cos_hi, sin_hi = cos_hi[:, None, :], sin_hi[:, None, :]
    cos_lo, sin_lo = cos_lo[None, :, :], sin_lo[None, :, :]
    cos_t = (cos_hi * cos_lo - sin_hi * sin_lo).reshape(half_len, -1)
    sin_t = (sin_hi * cos_lo + cos_hi * sin_lo).reshape(half_len, -1)
    return jnp.concatenate([cos_t, -sin_t], axis=0)


def whiten(spectrum, keep, half_len):
    power = jnp.sum(spectrum * spectrum, axis=-1, keepdims=True) / half_len
    return (spectrum * lax.rsqrt(power + 1e-06) * keep).astype(jnp.bfloat16)


def cross_spectrum(local, partner, half_len):
    real_a, imag_a = (local[..., :half_len], local[..., half_len:])
    real_b, imag_b = (partner[..., :half_len], partner[..., half_len:])
    real_sum = jnp.sum(real_a * real_b + imag_a * imag_b, axis=0)
    imag_sum = jnp.sum(imag_a * real_b - real_a * imag_b, axis=0)
    return jnp.concatenate([real_sum, imag_sum], axis=-1)


def pick_rows(rows, block):
    picks = (rows[:, None] == lax.iota(jnp.int32, block.shape[1])[None, :]).astype(block.dtype)
    return jnp.einsum("gp,spk->sgk", picks, block, preferred_element_type=jnp.float32)


def on_device(samples, offsets, bad_mask):
    channels, segments, length = samples.shape
    half_len = length // 2
    stops = offsets.shape[0]
    spectrum = jnp.dot(
        jnp.swapaxes(samples, 0, 1).reshape(segments * channels, length),
        forward_table(length),
        preferred_element_type=jnp.float32,
    ).reshape(segments, channels, length)
    keep = (1 - bad_mask).astype(jnp.float32)
    white = whiten(spectrum, keep[None, :, None], half_len)
    split = segments // 2
    ahead = white[:split]
    behind = white[split:]
    ahead_f32 = ahead.astype(jnp.float32)
    dc_imag = lax.broadcasted_iota(jnp.int32, behind.shape, 2) == half_len
    moving_ahead = ahead
    moving_behind = behind.at[:stops, :, half_len].set(offsets.astype(jnp.bfloat16))
    back_table = inverse_table(length, LAGS)

    def lags_of(stop, earlier, later):
        own = cross_spectrum(ahead_f32, pick_rows(offsets[stop - 1], earlier), half_len)
        later_offsets = later[stop - 1, :, half_len].astype(jnp.int32)
        later = jnp.where(dc_imag, jnp.zeros_like(later), later).astype(jnp.float32)
        later = cross_spectrum(later, pick_rows(later_offsets, behind), half_len)
        return jnp.concatenate([own, later], axis=0)

    def lags_of_stops(crosses):
        rows = crosses[0].shape[0]
        lags = jnp.dot(
            jnp.concatenate(crosses, axis=0),
            back_table,
            precision=lax.Precision.HIGH,
            preferred_element_type=jnp.float32,
        )
        return [lags[i * rows:(i + 1) * rows] for i in range(len(crosses))]

    near = stops // 2
    far_first = lax.optimization_barrier(
        tuple(shifted(moving_ahead, "blk", d) for d in range(near, 0, -1))
        + tuple(shifted(moving_behind, "blk", -d) for d in range(near, 0, -1))
    )
    first = far_first[:near][::-1] + far_first[near:][::-1]
    lags = [lags_of_stops([lags_of(d, first[d - 1], first[near + d - 1])])[0] for d in range(1, near + 1)]
    early = [
        (shifted(piece[channels:], "blk", d), shifted(piece[:channels], "blk", -d)) for d, piece in enumerate(lags, 1)
    ]
    far_ahead, far_behind, early = lax.optimization_barrier(
        (
            shifted(jnp.concatenate(first[:near], axis=0), "blk", near),
            shifted(jnp.concatenate(first[near:], axis=0), "blk", -near),
            early,
        )
    )
    lags += lags_of_stops(
        [
            lags_of(d, far_ahead[(d - near - 1) * split:(d - near) * split], far_behind[(d - near - 1) * split:(d - near) * split])
            for d in range(near + 1, stops + 1)
        ]
    )
    late = [(shifted(lags[d - 1][channels:], "blk", d), shifted(lags[d - 1][:channels], "blk", -d)) for d in
            range(near + 1, stops + 1)]
    own_parts = [piece[:channels] for piece in lags]
    later_parts = [piece[channels:] for piece in lags]
    from_earlier = [pair[0] for pair in early + late]
    from_later = [pair[1] for pair in early + late]
    corr_part = jnp.stack(own_parts, axis=1) + jnp.stack(from_earlier, axis=1)
    mirror_part = jnp.stack(from_later, axis=1) + jnp.stack(later_parts, axis=1)
    parts = jnp.stack([corr_part, mirror_part], axis=0)
    summed = parts + swapped(parts, "rep")
    scale = 1.0 / math.sqrt(segments * lax.axis_size("rep") * half_len)
    correlations = summed[0] * scale
    mirrored = (summed[1] * scale)[:, :, ::-1]
    return (correlations, mirrored)


def solution(mesh):
    return jax.shard_map(
        on_device,
        mesh=mesh,
        in_specs=(P("blk", "rep", None), P(None, "blk"), P("blk")),
        out_specs=(P("blk", None, None), P("blk", None, None)),
        check_vma=False,
    )
```

```python
import math

import jax
import jax.numpy as jnp
from jax import lax
from jax.sharding import PartitionSpec as P

LAGS = 128


def shifted(x, axis, by):
    length = lax.axis_size(axis)
    return lax.ppermute(x, axis, [(i, (i + by) % length) for i in range(length)])


def swapped(x, axis):
    length = lax.axis_size(axis)
    return lax.ppermute(x, axis, [(i, i ^ 1) for i in range(length)])


def cos_sin(phase, length):
    angle = phase.astype(jnp.float32) * (2.0 * math.pi / length)
    return jnp.cos(angle), jnp.sin(angle)


def forward_table(length):
    half_len = length // 2
    lo_len = 64
    hi_len = length // lo_len
    bin_idx = lax.iota(jnp.int32, half_len)
    hi_idx = lax.iota(jnp.int32, hi_len) * lo_len
    lo_idx = lax.iota(jnp.int32, lo_len)
    cos_hi, sin_hi = cos_sin(hi_idx[:, None] * bin_idx[None, :] % length, length)
    cos_lo, sin_lo = cos_sin(lo_idx[:, None] * bin_idx[None, :] % length, length)
    cos_hi, sin_hi = cos_hi[:, None, :], sin_hi[:, None, :]
    cos_lo, sin_lo = cos_lo[None, :, :], sin_lo[None, :, :]
    cos_t = cos_hi * cos_lo - sin_hi * sin_lo
    sin_t = sin_hi * cos_lo + cos_hi * sin_lo
    table = jnp.concatenate([cos_t, -sin_t], axis=-1)
    return table.reshape(length, length).astype(jnp.bfloat16)


def inverse_table(length, lag_half):
    half_len = length // 2
    lo_len = 32
    hi_len = half_len // lo_len
    lag_idx = (lax.iota(jnp.int32, 2 * lag_half + 1) - lag_half) % length
    hi_idx = lax.iota(jnp.int32, hi_len) * lo_len
    lo_idx = lax.iota(jnp.int32, lo_len)
    cos_hi, sin_hi = cos_sin(hi_idx[:, None] * lag_idx[None, :] % length, length)
    cos_lo, sin_lo = cos_sin(lo_idx[:, None] * lag_idx[None, :] % length, length)
    cos_hi, sin_hi = cos_hi[:, None, :], sin_hi[:, None, :]
    cos_lo, sin_lo = cos_lo[None, :, :], sin_lo[None, :, :]
    cos_t = (cos_hi * cos_lo - sin_hi * sin_lo).reshape(half_len, -1)
    sin_t = (sin_hi * cos_lo + cos_hi * sin_lo).reshape(half_len, -1)
    return jnp.concatenate([cos_t, -sin_t], axis=0)


def whiten(spectrum, keep, half_len):
    power = jnp.sum(spectrum * spectrum, axis=-1, keepdims=True) / half_len
    return (spectrum * lax.rsqrt(power + 1e-06) * keep).astype(jnp.bfloat16)


def cross_spectrum(local, partner, half_len):
    real_a, imag_a = (local[..., :half_len], local[..., half_len:])
    real_b, imag_b = (partner[..., :half_len], partner[..., half_len:])
    real_sum = jnp.sum(real_a * real_b + imag_a * imag_b, axis=0)
    imag_sum = jnp.sum(imag_a * real_b - real_a * imag_b, axis=0)
    return jnp.concatenate([real_sum, imag_sum], axis=-1)


def pick_rows(rows, block):
    picks = (rows[:, None] == lax.iota(jnp.int32, block.shape[1])[None, :]).astype(block.dtype)
    return jnp.einsum("gp,spk->sgk", picks, block, preferred_element_type=jnp.float32)


def on_device(samples, offsets, bad_mask):
    channels, segments, length = samples.shape
    half_len = length // 2
    stops = offsets.shape[0]
    spectrum = jnp.dot(
        jnp.swapaxes(samples, 0, 1).reshape(segments * channels, length),
        forward_table(length),
        preferred_element_type=jnp.float32,
    ).reshape(segments, channels, length)
    keep = (1 - bad_mask).astype(jnp.float32)
    white = whiten(spectrum, keep[None, :, None], half_len)
    split = segments // 2
    ahead = white[:split]
    behind = white[split:]
    ahead_f32 = ahead.astype(jnp.float32)
    dc_imag = lax.broadcasted_iota(jnp.int32, behind.shape, 2) == half_len
    moving_ahead = ahead
    moving_behind = behind.at[:stops, :, half_len].set(offsets.astype(jnp.bfloat16))
    back_table = inverse_table(length, LAGS)

    def lags_of(stop, earlier, later):
        own = cross_spectrum(ahead_f32, pick_rows(offsets[stop - 1], earlier), half_len)
        later_offsets = later[stop - 1, :, half_len].astype(jnp.int32)
        later = jnp.where(dc_imag, jnp.zeros_like(later), later).astype(jnp.float32)
        later = cross_spectrum(later, pick_rows(later_offsets, behind), half_len)
        return jnp.concatenate([own, later], axis=0)

    def lags_of_stops(crosses):
        rows = crosses[0].shape[0]
        lags = jnp.dot(
            jnp.concatenate(crosses, axis=0),
            back_table,
            precision=lax.Precision.HIGH,
            preferred_element_type=jnp.float32,
        )
        return [lags[i * rows:(i + 1) * rows] for i in range(len(crosses))]

    near = stops // 2
    far_first = lax.optimization_barrier(
        tuple(shifted(moving_ahead, "blk", d) for d in range(near, 0, -1))
        + tuple(shifted(moving_behind, "blk", -d) for d in range(near, 0, -1))
    )
    first = far_first[:near][::-1] + far_first[near:][::-1]
    lags = [lags_of_stops([lags_of(d, first[d - 1], first[near + d - 1])])[0] for d in range(1, near + 1)]
    early = [
        (shifted(piece[channels:], "blk", d), shifted(piece[:channels], "blk", -d)) for d, piece in enumerate(lags, 1)
    ]
    far_behind, far_ahead, early = lax.optimization_barrier(
        (
            shifted(jnp.concatenate(first[near:], axis=0), "blk", -near),
            shifted(jnp.concatenate(first[:near], axis=0), "blk", near),
            early,
        )
    )
    lags += lags_of_stops(
        [
            lags_of(d, far_ahead[(d - near - 1) * split:(d - near) * split], far_behind[(d - near - 1) * split:(d - near) * split])
            for d in range(near + 1, stops + 1)
        ]
    )
    late = [(shifted(lags[d - 1][channels:], "blk", d), shifted(lags[d - 1][:channels], "blk", -d)) for d in
            range(near + 1, stops + 1)]
    own_parts = [piece[:channels] for piece in lags]
    later_parts = [piece[channels:] for piece in lags]
    from_earlier = [pair[0] for pair in early + late]
    from_later = [pair[1] for pair in early + late]
    corr_part = jnp.stack(own_parts, axis=1) + jnp.stack(from_earlier, axis=1)
    mirror_part = jnp.stack(from_later, axis=1) + jnp.stack(later_parts, axis=1)
    parts = jnp.stack([corr_part, mirror_part], axis=0)
    summed = parts + swapped(parts, "rep")
    scale = 1.0 / math.sqrt(segments * lax.axis_size("rep") * half_len)
    correlations = summed[0] * scale
    mirrored = (summed[1] * scale)[:, :, ::-1]
    return (correlations, mirrored)


def solution(mesh):
    return jax.shard_map(
        on_device,
        mesh=mesh,
        in_specs=(P("blk", "rep", None), P(None, "blk"), P("blk")),
        out_specs=(P("blk", None, None), P("blk", None, None)),
        check_vma=False,
    )
```

```python
import math

import jax
import jax.numpy as jnp
from jax import lax
from jax.sharding import PartitionSpec as P

LAGS = 128


def shifted(x, axis, by):
    length = lax.axis_size(axis)
    return lax.ppermute(x, axis, [(i, (i + by) % length) for i in range(length)])


def swapped(x, axis):
    length = lax.axis_size(axis)
    return lax.ppermute(x, axis, [(i, i ^ 1) for i in range(length)])


def cos_sin(phase, length):
    angle = phase.astype(jnp.float32) * (2.0 * math.pi / length)
    return jnp.cos(angle), jnp.sin(angle)


def forward_table(length):
    half_len = length // 2
    lo_len = 64
    hi_len = length // lo_len
    bin_idx = lax.iota(jnp.int32, half_len)
    hi_idx = lax.iota(jnp.int32, hi_len) * lo_len
    lo_idx = lax.iota(jnp.int32, lo_len)
    cos_hi, sin_hi = cos_sin(hi_idx[:, None] * bin_idx[None, :] % length, length)
    cos_lo, sin_lo = cos_sin(lo_idx[:, None] * bin_idx[None, :] % length, length)
    cos_hi, sin_hi = cos_hi[:, None, :], sin_hi[:, None, :]
    cos_lo, sin_lo = cos_lo[None, :, :], sin_lo[None, :, :]
    cos_t = cos_hi * cos_lo - sin_hi * sin_lo
    sin_t = sin_hi * cos_lo + cos_hi * sin_lo
    table = jnp.concatenate([cos_t, -sin_t], axis=-1)
    return table.reshape(length, length).astype(jnp.bfloat16)


def inverse_table(length, lag_half):
    half_len = length // 2
    lo_len = 32
    hi_len = half_len // lo_len
    lag_idx = (lax.iota(jnp.int32, 2 * lag_half + 1) - lag_half) % length
    hi_idx = lax.iota(jnp.int32, hi_len) * lo_len
    lo_idx = lax.iota(jnp.int32, lo_len)
    cos_hi, sin_hi = cos_sin(hi_idx[:, None] * lag_idx[None, :] % length, length)
    cos_lo, sin_lo = cos_sin(lo_idx[:, None] * lag_idx[None, :] % length, length)
    cos_hi, sin_hi = cos_hi[:, None, :], sin_hi[:, None, :]
    cos_lo, sin_lo = cos_lo[None, :, :], sin_lo[None, :, :]
    cos_t = (cos_hi * cos_lo - sin_hi * sin_lo).reshape(half_len, -1)
    sin_t = (sin_hi * cos_lo + cos_hi * sin_lo).reshape(half_len, -1)
    return jnp.concatenate([cos_t, -sin_t], axis=0)


def whiten(spectrum, keep, half_len):
    power = jnp.sum(spectrum * spectrum, axis=-1, keepdims=True) / half_len
    return (spectrum * lax.rsqrt(power + 1e-06) * keep).astype(jnp.bfloat16)


def cross_spectrum(local, partner, half_len):
    real_a, imag_a = (local[..., :half_len], local[..., half_len:])
    real_b, imag_b = (partner[..., :half_len], partner[..., half_len:])
    real_sum = jnp.sum(real_a * real_b + imag_a * imag_b, axis=0)
    imag_sum = jnp.sum(imag_a * real_b - real_a * imag_b, axis=0)
    return jnp.concatenate([real_sum, imag_sum], axis=-1)


def pick_rows(rows, block):
    picks = (rows[:, None] == lax.iota(jnp.int32, block.shape[1])[None, :]).astype(block.dtype)
    return jnp.einsum("gp,spk->sgk", picks, block, preferred_element_type=jnp.float32)


def on_device(samples, offsets, bad_mask):
    channels, segments, length = samples.shape
    half_len = length // 2
    stops = offsets.shape[0]
    spectrum = jnp.einsum("csn,nk->sck", samples, forward_table(length), preferred_element_type=jnp.float32)
    keep = (1 - bad_mask).astype(jnp.float32)
    white = whiten(spectrum, keep[None, :, None], half_len)
    split = segments // 2
    ahead = white[:split]
    behind = white[split:]
    ahead_f32 = ahead.astype(jnp.float32)
    dc_imag = lax.broadcasted_iota(jnp.int32, behind.shape, 2) == half_len
    moving_ahead = ahead
    moving_behind = behind.at[:stops, :, half_len].set(offsets.astype(jnp.bfloat16))
    back_table = inverse_table(length, LAGS)

    def lags_of(stop, earlier, later):
        own = cross_spectrum(ahead_f32, pick_rows(offsets[stop - 1], earlier), half_len)
        later_offsets = later[stop - 1, :, half_len].astype(jnp.int32)
        later = jnp.where(dc_imag, jnp.zeros_like(later), later).astype(jnp.float32)
        later = cross_spectrum(later, pick_rows(later_offsets, behind), half_len)
        return jnp.concatenate([own, later], axis=0)

    def lags_of_stops(crosses):
        rows = crosses[0].shape[0]
        lags = jnp.dot(
            jnp.concatenate(crosses, axis=0),
            back_table,
            precision=lax.Precision.HIGH,
            preferred_element_type=jnp.float32,
        )
        return [lags[i * rows:(i + 1) * rows] for i in range(len(crosses))]

    near = stops // 2
    far_first = lax.optimization_barrier(
        tuple(shifted(moving_ahead, "blk", d) for d in range(near, 0, -1))
        + tuple(shifted(moving_behind, "blk", -d) for d in range(near, 0, -1))
    )
    first = far_first[:near][::-1] + far_first[near:][::-1]
    lags = [lags_of_stops([lags_of(d, first[d - 1], first[near + d - 1])])[0] for d in range(1, near + 1)]
    early = [
        (shifted(piece[channels:], "blk", d), shifted(piece[:channels], "blk", -d)) for d, piece in enumerate(lags, 1)
    ]
    far_ahead, far_behind, early = lax.optimization_barrier(
        (
            shifted(jnp.concatenate(first[:near], axis=0), "blk", near),
            shifted(jnp.concatenate(first[near:], axis=0), "blk", -near),
            early,
        )
    )
    lags += lags_of_stops(
        [
            lags_of(d, far_ahead[(d - near - 1) * split:(d - near) * split], far_behind[(d - near - 1) * split:(d - near) * split])
            for d in range(near + 1, stops + 1)
        ]
    )
    late = [(shifted(lags[d - 1][channels:], "blk", d), shifted(lags[d - 1][:channels], "blk", -d)) for d in
            range(near + 1, stops + 1)]
    own_parts = [piece[:channels] for piece in lags]
    later_parts = [piece[channels:] for piece in lags]
    from_earlier = [pair[0] for pair in early + late]
    from_later = [pair[1] for pair in early + late]
    corr_part = jnp.stack(own_parts, axis=1) + jnp.stack(from_earlier, axis=1)
    mirror_part = jnp.stack(from_later, axis=1) + jnp.stack(later_parts, axis=1)
    parts = jnp.stack([corr_part, mirror_part], axis=0)
    summed = parts + swapped(parts, "rep")
    scale = 1.0 / math.sqrt(segments * lax.axis_size("rep") * half_len)
    correlations = summed[0] * scale
    mirrored = (summed[1] * scale)[:, :, ::-1]
    return (correlations, mirrored)


def solution(mesh):
    return jax.shard_map(
        on_device,
        mesh=mesh,
        in_specs=(P("blk", "rep", None), P(None, "blk"), P("blk")),
        out_specs=(P("blk", None, None), P("blk", None, None)),
        check_vma=False,
    )
```
